128 devices in a mesh: ctx: 16 (over x, z), tp: 8 (over y, core).
Axes of the slice: x: 4, y: 4, z: 4, core: 2. Of those that a mesh axis runs over, the one named last changes fastest.
Arguments:
- ssm_input: bfloat16 [8192, 16384], P('ctx', 'tp'), may hold values from -6 to 6
- gate_input: bfloat16 [8192, 16384], P('ctx', 'tp'), may hold values from -6 to 6
- state_maps: bfloat16 [8192, 2, 1024], P('ctx', None, 'tp'), may hold values from -6 to 6
- step_size: float32 [8192, 256], P('ctx', 'tp'), may hold values from 0 to 8, as said below
- decay_rate: float32 [256], P('tp'), may hold values from 0 to 1, as said below
- skip_gain: float32 [256], P('tp'), may hold values from 0.5 to 1.5
- conv_weight: float32 [4, 16384], P(None, 'tp'), may hold values from -0.5 to 0.5
- conv_bias: float32 [16384], P('tp'), may hold values from -0.5 to 0.5
- map_conv: float32 [4, 2, 1024], P(None, None, 'tp'), may hold values from -0.5 to 0.5
- map_bias: float32 [2, 1024], P(None, 'tp'), may hold values from -1 to 1
- norm_gain: float32 [16384], P('tp'), may hold values from 0.1 to 1.9
- out_weight: bfloat16 [16384, 4096], P('tp'), may hold values from -0.046875 to 0.046875
Outputs:
- mixer_out: bfloat16 [8192, 4096], P(('ctx', 'tp'))
The draws below stay inside these ranges and needn't reach their ends.
Inputs may be any that keep to these rules, and one draw needn't show every extreme that they name: `step_size`: positive step of every token and head. `decay_rate`: positive rate of every head.
All inputs are finite; a program needn't handle non-finite values.
Results may differ from the reference program's by a relative error of at most 0.03.
Values may be sent and summed in bfloat16 or wider, within the bound.
No kernel may reach another device: no remote copies, remote signals or barrier semaphores. Data moves between devices by JAX's collectives and lax.ppermute only.
A program may use at most 192 MiB of HBM per device.

```python
import math
import jax
import jax.numpy as jnp
from jax import lax

MIXER_HEADS = 256
HEAD_DIM = 64
STATE = 128
GROUPS = 8
CONV = 4
BLOCK = 128
D_OUT = 4096
TOK_DEV = 512
D_INNER = 16384
SEQUENCE_TOKENS = 8192
N_TP = 8


def decay_tables(key):
    base_key = jax.random.fold_in(key, 4099)
    random_keys = jax.random.split(base_key, 8)
    slow_share = 0.5
    slow_flag = jax.random.uniform(random_keys[1], (MIXER_HEADS,), jnp.float32) < slow_share
    slow_total = jnp.exp(jax.random.uniform(random_keys[2], (MIXER_HEADS,), jnp.float32, math.log(0.05), math.log(0.3)))
    slow_rate = slow_total / SEQUENCE_TOKENS
    fast_reach = jnp.exp(jax.random.uniform(random_keys[3], (MIXER_HEADS,), jnp.float32, math.log(30.0), math.log(50.0)))
    per_token = jnp.where(slow_flag, slow_rate, 1.0 / fast_reach)
    head_rate = per_token / 0.5
    block_factor = jnp.exp(jax.random.uniform(random_keys[4], (SEQUENCE_TOKENS // TOK_DEV,), jnp.float32, math.log(0.6), math.log(1.5)))
    block_factor = jnp.repeat(block_factor, TOK_DEV)
    roughness = jax.random.uniform(random_keys[5], (SEQUENCE_TOKENS, MIXER_HEADS), jnp.float32, 0.5, 1.5)
    steps = 0.5 * block_factor[:, None] * roughness
    spike_rows = jax.random.randint(random_keys[6], (2,), 0, SEQUENCE_TOKENS)
    spike_loss = jax.random.uniform(random_keys[7], (2, MIXER_HEADS), jnp.float32, 0.22, 0.69)
    spike_steps = jnp.minimum(spike_loss / head_rate[None, :], 8.0)
    token_places = jnp.arange(SEQUENCE_TOKENS)
    steps = jnp.where((token_places == spike_rows[0])[:, None], spike_steps[0][None, :], steps)
    steps = jnp.where((token_places == spike_rows[1])[:, None], spike_steps[1][None, :], steps)
    return (head_rate, steps)


def draw_decay_rate(key, part):
    return decay_tables(key)[0]


def draw_step_size(key, part):
    return decay_tables(key)[1]


def level_of(key, extent, shards, smallest, high):
    def one(position, parts):
        heights = jax.random.uniform(jax.random.fold_in(jax.random.fold_in(key, 6), position), (parts,), jnp.float32, smallest / len(shards), high / len(shards))
        return jnp.repeat(jnp.exp(heights), extent[position] // parts).reshape((-1,) + (1,) * (len(extent) - position - 1))

    loudness = one(*shards[0])
    for cut in shards[1:]:
        loudness = loudness * one(*cut)
    return loudness


def gaussian(own_key, extent, scale, most, cuts=(), kind=jnp.bfloat16):
    result = scale * jax.random.normal(own_key, extent, jnp.float32)
    if cuts:
        result = result * level_of(own_key, extent, cuts, -0.22, 0.18)
    return jnp.clip(result, -most, most).astype(kind)


def setup_inputs(seed: int = 0) -> dict:
    splits = jax.random.split(jax.random.key(seed), 13)
    ssm_input = gaussian(splits[0], (SEQUENCE_TOKENS, D_INNER), 1.0, 6.0, ((0, 16), (1, 8)))
    gate_input = gaussian(splits[1], (SEQUENCE_TOKENS, D_INNER), 1.0, 6.0, ((0, 16), (1, 8)))
    state_maps = gaussian(splits[2], (SEQUENCE_TOKENS, 2, GROUPS * STATE), 1.0, 6.0, ((0, 16), (2, 8)))
    step_size = draw_step_size(jax.random.fold_in(splits[12], 71), 0)
    decay_rate = draw_decay_rate(jax.random.fold_in(splits[12], 71), 0)
    skip_gain = jnp.clip(0.5 + 1.0 * jax.random.uniform(splits[5], (MIXER_HEADS,), jnp.float32) ** level_of(splits[5], (MIXER_HEADS,), ((0, 8),), -0.2, 0.2), 0.5, 1.5)
    conv_weight = jnp.clip(jax.random.uniform(splits[6], (CONV, D_INNER), jnp.float32, -0.5, 0.5) * level_of(splits[6], (CONV, D_INNER), ((1, 8),), -0.4, 0.0), -0.5, 0.5)
    conv_bias = jnp.clip(jax.random.uniform(splits[7], (D_INNER,), jnp.float32, -0.5, 0.5) * level_of(splits[7], (D_INNER,), ((0, 8),), -0.4, 0.0), -0.5, 0.5)
    map_conv = jnp.clip(jax.random.uniform(splits[8], (CONV, 2, GROUPS * STATE), jnp.float32, -0.5, 0.5) * level_of(splits[8], (CONV, 2, GROUPS * STATE), ((2, 8),), -0.4, 0.0), -0.5, 0.5)
    map_bias = jnp.clip(jax.random.uniform(splits[9], (2, GROUPS * STATE), jnp.float32, -1.0, 1.0) * level_of(splits[9], (2, GROUPS * STATE), ((1, 8),), -0.4, 0.0), -1.0, 1.0)
    norm_gain = jnp.clip(1.0 + 0.18 * jax.random.normal(splits[10], (D_INNER,), jnp.float32), 0.1, 1.9)
    out_weight = gaussian(splits[11], (D_INNER, D_OUT), D_INNER ** -0.5, 0.046875, ((0, 8),))
    return {"ssm_input": ssm_input, "gate_input": gate_input, "state_maps": state_maps, "step_size": step_size, "decay_rate": decay_rate, "skip_gain": skip_gain, "conv_weight": conv_weight, "conv_bias": conv_bias, "map_conv": map_conv, "map_bias": map_bias, "norm_gain": norm_gain, "out_weight": out_weight}


def rounded(values):
    return lax.optimization_barrier(values.astype(jnp.bfloat16))

def causal_conv(values, weight, bias_term):
    lead_rows = jnp.zeros((CONV - 1,) + values.shape[1:], values.dtype)
    padded = jnp.concatenate([lead_rows, values], axis=0)
    length = values.shape[0]
    accum = jnp.zeros(values.shape, jnp.float32) + bias_term.astype(jnp.float32)
    for offset in range(CONV):
        accum = accum + weight[offset].astype(jnp.float32) * padded[offset:offset + length].astype(jnp.float32)
    return rounded(jax.nn.silu(accum))

def reference(ssm_input, gate_input, state_maps, step_size, decay_rate, skip_gain, conv_weight, conv_bias, map_conv, map_bias, norm_gain, out_weight):
    conv_out = causal_conv(ssm_input, conv_weight, conv_bias)
    maps_out = causal_conv(state_maps, map_conv, map_bias)
    repeat = MIXER_HEADS // GROUPS
    blocks = SEQUENCE_TOKENS // BLOCK
    inner_width = MIXER_HEADS * HEAD_DIM
    log_decay = -decay_rate[None, :] * step_size
    values = conv_out.reshape(blocks, BLOCK, MIXER_HEADS, HEAD_DIM)
    input_maps = maps_out[:, 0].reshape(blocks, BLOCK, GROUPS, STATE)
    output_maps = maps_out[:, 1].reshape(blocks, BLOCK, GROUPS, STATE)
    block_logs = log_decay.reshape(blocks, BLOCK, MIXER_HEADS)
    block_steps = step_size.reshape(blocks, BLOCK, MIXER_HEADS)
    gate_blocks = gate_input.reshape(blocks, BLOCK, inner_width)
    causal_mask = jnp.tril(jnp.ones((BLOCK, BLOCK), dtype=bool))

    def block_step(carry_state, inputs):
        block_values, input_map, output_map, log_block, step_block, gate_block = inputs
        running = jnp.cumsum(log_block, axis=0)
        scores = jnp.einsum('qgn,sgn->gqs', output_map.astype(jnp.float32), input_map.astype(jnp.float32))
        scores = jnp.repeat(scores, repeat, axis=0)
        head_major = running.T
        gap_log = head_major[:, :, None] - head_major[:, None, :]
        decays = jnp.exp(jnp.where(causal_mask[None], gap_log, -1e+30))
        weights = rounded(scores * decays * step_block.T[:, None, :])
        within = jnp.einsum('hqs,shp->qhp', weights.astype(jnp.float32), block_values.astype(jnp.float32))
        to_end = jnp.exp(running[-1][None, :] - running) * step_block
        input_heads = jnp.repeat(input_map, repeat, axis=1)
        loaded = rounded(input_heads.astype(jnp.float32) * to_end[:, :, None])
        fresh_state = jnp.einsum('shn,shp->hnp', loaded.astype(jnp.float32), block_values.astype(jnp.float32))
        carried = rounded(carry_state)
        output_heads = jnp.repeat(output_map, repeat, axis=1)
        before = jnp.exp(running)[:, :, None] * jnp.einsum('qhn,hnp->qhp', output_heads.astype(jnp.float32), carried.astype(jnp.float32))
        output = within + before + skip_gain[None, :, None] * block_values.astype(jnp.float32)
        gated = output.reshape(BLOCK, inner_width) * jax.nn.silu(gate_block.astype(jnp.float32))
        grouped = gated.reshape(BLOCK, GROUPS, inner_width // GROUPS)
        inverse_rms = lax.rsqrt(lax.optimization_barrier(jnp.mean(grouped * grouped, axis=2, keepdims=True)) + 1e-05)
        normed = (grouped * inverse_rms).reshape(BLOCK, inner_width) * norm_gain[None, :]
        new_state = jnp.exp(running[-1])[:, None, None] * carry_state + fresh_state
        return (new_state, normed.astype(jnp.bfloat16))
    initial = jnp.zeros((MIXER_HEADS, STATE, HEAD_DIM), jnp.float32)
    final_state, normed = lax.scan(block_step, initial, (values, input_maps, output_maps, block_logs, block_steps, gate_blocks))
    normed = normed.reshape(SEQUENCE_TOKENS, inner_width)
    share_width = inner_width // N_TP
    summed = jnp.zeros((SEQUENCE_TOKENS, D_OUT), jnp.float32)
    for block_index in range(N_TP):
        lower = block_index * share_width
        partial_sum = jnp.dot(normed[:, lower:lower + share_width].astype(jnp.float32), out_weight[lower:lower + share_width].astype(jnp.float32), preferred_element_type=jnp.float32)
        summed = summed + rounded(partial_sum).astype(jnp.float32)
    return summed.astype(jnp.bfloat16)
```

```python
import jax
import jax.numpy as jnp
from jax import lax
from jax.sharding import PartitionSpec as P

HEAD_DIM = 64
STATE = 128
CONV = 4
BLOCK = 128


def passed_along(value, axis, steps):
    count = lax.axis_size(axis)
    first, last = (max(0, -steps), min(count, count - steps))
    return lax.ppermute(value, axis, [(source, source + steps) for source in range(first, last)])


def exclusive_scan(log_total, state, axis):
    count = lax.axis_size(axis)
    window_log, window_state = log_total, state
    prior_log = jnp.zeros_like(log_total)
    prior_state = jnp.zeros_like(state)
    distance = 1
    while distance < count:
        pairs = [(source, source + distance) for source in range(count - distance)]
        got_log = lax.ppermute(window_log, axis, pairs)
        got_state = lax.ppermute(window_state.astype(jnp.bfloat16), axis, pairs).astype(jnp.float32)
        prior_state = jnp.exp(prior_log)[:, None, None] * got_state + prior_state
        prior_log = got_log + prior_log
        if 2 * distance < count:
            window_state = jnp.exp(window_log)[:, None, None] * got_state + window_state
            window_log = got_log + window_log
        distance *= 2
    return prior_log, prior_state


def scattered_sum(rows, weight, axis):
    count = lax.axis_size(axis)
    chips = count // 2
    place = lax.axis_index(axis)
    core = place % 2
    chip = place // 2
    length = rows.shape[0]
    share = length // count
    width = weight.shape[1]
    blocks = rows.reshape(chips, 2, share, rows.shape[1])
    sent_rows = lax.dynamic_index_in_dim(blocks, 1 - core, 1, False)
    kept_rows = lax.dynamic_index_in_dim(blocks, core, 1, False)
    sent = jnp.einsum("ysk,kd->ysd", sent_rows, weight, preferred_element_type=jnp.float32)
    swapped = lax.ppermute(
        sent.astype(jnp.bfloat16), axis, [(source, source ^ 1) for source in range(count)]
    )
    kept = jnp.einsum("ysk,kd->ysd", kept_rows, weight, preferred_element_type=jnp.float32)
    summed = kept + swapped.astype(jnp.float32)
    if chips == 1:
        return summed[0].astype(jnp.bfloat16)
    half = width // 2
    rightward = [(source, (source + 2) % count) for source in range(count)]
    leftward = [(source, (source - 2) % count) for source in range(count)]
    right_acc = lax.dynamic_index_in_dim(summed, (chip - 1) % chips, 0, False)[:, :half]
    left_acc = lax.dynamic_index_in_dim(summed, (chip + 1) % chips, 0, False)[:, half:]
    for step in range(chips - 1):
        got_right = lax.ppermute(right_acc.astype(jnp.bfloat16), axis, rightward)
        got_left = lax.ppermute(left_acc.astype(jnp.bfloat16), axis, leftward)
        right_own = lax.dynamic_index_in_dim(summed, (chip - 2 - step) % chips, 0, False)[:, :half]
        left_own = lax.dynamic_index_in_dim(summed, (chip + 2 + step) % chips, 0, False)[:, half:]
        right_acc = right_own + got_right.astype(jnp.float32)
        left_acc = left_own + got_left.astype(jnp.float32)
    return jnp.concatenate([right_acc, left_acc], axis=1).astype(jnp.bfloat16)


def causal_conv(values, lead_rows, weight, bias_term):
    padded = jnp.concatenate([lead_rows, values], axis=0)
    length = values.shape[0]
    accum = jnp.zeros(values.shape, jnp.float32) + bias_term
    for offset in range(weight.shape[0]):
        accum = accum + weight[offset] * padded[offset : offset + length].astype(jnp.float32)
    return jax.nn.silu(accum).astype(jnp.bfloat16)


def local(
    ssm_input,
    gate_input,
    state_maps,
    step_size,
    decay_rate,
    skip_gain,
    conv_weight,
    conv_bias,
    map_conv,
    map_bias,
    norm_gain,
    out_weight,
):
    length = ssm_input.shape[0]
    head_count = step_size.shape[1]
    inner_width = ssm_input.shape[1]
    groups = state_maps.shape[2] // STATE
    repeat = head_count // groups
    blocks = length // BLOCK
    lead_input, lead_maps = passed_along(
        (ssm_input[length - CONV + 1 :], state_maps[length - CONV + 1 :]), "ctx", 1
    )
    conv_out = causal_conv(ssm_input, lead_input, conv_weight, conv_bias)
    maps_out = causal_conv(state_maps, lead_maps, map_conv, map_bias)
    log_decay = -decay_rate[None, :] * step_size
    running = jnp.cumsum(log_decay.reshape(blocks, BLOCK, head_count), axis=1)
    values = conv_out.reshape(blocks, BLOCK, head_count, HEAD_DIM)
    input_maps = maps_out[:, 0].reshape(blocks, BLOCK, groups, STATE)
    output_maps = maps_out[:, 1].reshape(blocks, BLOCK, groups, STATE)
    block_steps = step_size.reshape(blocks, BLOCK, head_count)
    scores = jnp.einsum(
        "cqgn,csgn->cgqs", output_maps, input_maps, preferred_element_type=jnp.float32
    )
    scores = jnp.broadcast_to(scores[:, :, None], (blocks, groups, repeat, BLOCK, BLOCK)).reshape(
        blocks, head_count, BLOCK, BLOCK
    )
    head_major = jnp.transpose(running, (0, 2, 1))
    gap_log = head_major[:, :, :, None] - head_major[:, :, None, :]
    causal_mask = jnp.tril(jnp.ones((BLOCK, BLOCK), dtype=bool))
    decays = jnp.exp(jnp.where(causal_mask[None, None], gap_log, -1e30))
    step_major = jnp.transpose(block_steps, (0, 2, 1))
    weights = (scores * decays * step_major[:, :, None, :]).astype(jnp.bfloat16)
    within = jnp.einsum("chqs,cshp->cqhp", weights, values, preferred_element_type=jnp.float32)
    to_end = jnp.exp(running[:, -1:, :] - running) * block_steps
    input_heads = jnp.broadcast_to(
        input_maps[:, :, :, None], (blocks, BLOCK, groups, repeat, STATE)
    ).reshape(blocks, BLOCK, head_count, STATE)
    loaded = (input_heads.astype(jnp.float32) * to_end[..., None]).astype(jnp.bfloat16)
    fresh_state = jnp.einsum("cshn,cshp->chnp", loaded, values, preferred_element_type=jnp.float32)
    totals = running[:, -1, :]

    empty_state = jnp.zeros((head_count, STATE, HEAD_DIM), jnp.float32)
    local_enter = []
    carry_state = empty_state
    for block in range(blocks):
        local_enter.append(carry_state)
        carry_state = jnp.exp(totals[block])[:, None, None] * carry_state + fresh_state[block]
    local_end = carry_state
    local_enter = jnp.stack(local_enter)
    device_log = jnp.sum(totals, axis=0)
    before_log, incoming = exclusive_scan(device_log, local_end, "ctx")
    prior_log = jnp.cumsum(totals, axis=0) - totals
    entering = jnp.exp(prior_log)[:, :, None, None] * incoming[None] + local_enter
    carried = entering.astype(jnp.bfloat16).reshape(blocks, groups, repeat, STATE, HEAD_DIM)
    before = jnp.einsum(
        "cqgn,cgrnp->cqgrp", output_maps, carried, preferred_element_type=jnp.float32
    )
    before = jnp.exp(running)[..., None] * before.reshape(blocks, BLOCK, head_count, HEAD_DIM)
    output = within + before + skip_gain[None, None, :, None] * values.astype(jnp.float32)
    gated = output.reshape(length, inner_width) * jax.nn.silu(gate_input.astype(jnp.float32))
    grouped = gated.reshape(length, groups, inner_width // groups)
    inverse_rms = lax.rsqrt(jnp.mean(grouped * grouped, axis=2, keepdims=True) + 1e-05)
    normed = ((grouped * inverse_rms).reshape(length, inner_width) * norm_gain[None, :]).astype(
        jnp.bfloat16
    )
    return scattered_sum(normed, out_weight, "tp")


def solution(mesh):
    in_specs = (
        P("ctx", "tp"),
        P("ctx", "tp"),
        P("ctx", None, "tp"),
        P("ctx", "tp"),
        P("tp"),
        P("tp"),
        P(None, "tp"),
        P("tp"),
        P(None, None, "tp"),
        P(None, "tp"),
        P("tp"),
        P("tp", None),
    )
    out_specs = P(("ctx", "tp"), None)
    return jax.shard_map(local, mesh=mesh, in_specs=in_specs, out_specs=out_specs, check_vma=False)
```

```python
import jax
import jax.numpy as jnp
from jax import lax
from jax.sharding import PartitionSpec as P

HEAD_DIM = 64
STATE = 128
CONV = 4
BLOCK = 128


def passed_along(value, axis, steps):
    count = lax.axis_size(axis)
    first, last = (max(0, -steps), min(count, count - steps))
    return lax.ppermute(value, axis, [(source, source + steps) for source in range(first, last)])


def exclusive_scan(log_total, state, axis):
    count = lax.axis_size(axis)
    heads = state.shape[0]
    window_log, window_state = log_total, state
    prior_log = jnp.zeros_like(log_total)
    prior_state = jnp.zeros_like(state)
    distance = 1
    while distance < count:
        pairs = [(source, source + distance) for source in range(count - distance)]
        high = window_log.astype(jnp.bfloat16)
        low = (window_log - high.astype(jnp.float32)).astype(jnp.bfloat16)
        log_rows = jnp.zeros((1,) + state.shape[1:], jnp.bfloat16)
        log_rows = log_rows.at[0, :heads, 0].set(high).at[0, :heads, 1].set(low)
        packed = jnp.concatenate([window_state.astype(jnp.bfloat16), log_rows], axis=0)
        got = lax.ppermute(packed, axis, pairs)
        got_state = got[:heads].astype(jnp.float32)
        got_log = got[heads, :heads, 0].astype(jnp.float32) + got[heads, :heads, 1].astype(jnp.float32)
        prior_state = jnp.exp(prior_log)[:, None, None] * got_state + prior_state
        prior_log = got_log + prior_log
        if 2 * distance < count:
            window_state = jnp.exp(window_log)[:, None, None] * got_state + window_state
            window_log = got_log + window_log
        distance *= 2
    return prior_log, prior_state


def scattered_sum(rows, weight, axis):
    count = lax.axis_size(axis)
    chips = count // 2
    place = lax.axis_index(axis)
    core = place % 2
    chip = place // 2
    share = rows.shape[0] // count
    half = weight.shape[1] // 2
    blocks = rows.reshape(chips, 2, share, rows.shape[1])
    weight_right, weight_left = weight[:, :half], weight[:, half:]

    def rows_of(block, which_core):
        chosen = lax.dynamic_index_in_dim(blocks, block % chips, 0, False)
        return lax.dynamic_index_in_dim(chosen, which_core, 0, False)

    def piece(step, which_core):
        right = jnp.dot(rows_of(chip - 1 - step, which_core), weight_right, preferred_element_type=jnp.float32)
        left = jnp.dot(rows_of(chip + 1 + step, which_core), weight_left, preferred_element_type=jnp.float32)
        return right, left

    swap = [(source, source ^ 1) for source in range(count)]
    summed = []
    for step in range(chips):
        sent_right, sent_left = piece(step, 1 - core)
        got = lax.ppermute(jnp.stack([sent_right, sent_left]).astype(jnp.bfloat16), axis, swap)
        kept_right, kept_left = piece(step, core)
        summed.append((kept_right + got[0].astype(jnp.float32), kept_left + got[1].astype(jnp.float32)))
    right_acc, left_acc = summed[0]
    rightward = [(source, (source + 2) % count) for source in range(count)]
    leftward = [(source, (source - 2) % count) for source in range(count)]
    for step in range(chips - 1):
        got_right = lax.ppermute(right_acc.astype(jnp.bfloat16), axis, rightward)
        got_left = lax.ppermute(left_acc.astype(jnp.bfloat16), axis, leftward)
        right_acc = summed[step + 1][0] + got_right.astype(jnp.float32)
        left_acc = summed[step + 1][1] + got_left.astype(jnp.float32)
    return jnp.concatenate([right_acc, left_acc], axis=1).astype(jnp.bfloat16)


def causal_conv(values, lead_rows, weight, bias_term):
    padded = lax.optimization_barrier(
        jnp.concatenate([lead_rows, values], axis=0).astype(jnp.float32)
    )
    length = values.shape[0]
    accum = jnp.zeros(values.shape, jnp.float32) + bias_term
    for offset in range(weight.shape[0]):
        accum = accum + weight[offset] * padded[offset : offset + length]
    return jax.nn.silu(accum).astype(jnp.bfloat16)


def local(
    ssm_input,
    gate_input,
    state_maps,
    step_size,
    decay_rate,
    skip_gain,
    conv_weight,
    conv_bias,
    map_conv,
    map_bias,
    norm_gain,
    out_weight,
):
    length = ssm_input.shape[0]
    head_count = step_size.shape[1]
    inner_width = ssm_input.shape[1]
    groups = state_maps.shape[2] // STATE
    repeat = head_count // groups
    blocks = length // BLOCK
    map_width = state_maps.shape[1] * state_maps.shape[2]
    lead_both = passed_along(
        jnp.concatenate(
            [
                ssm_input[length - CONV + 1 :],
                state_maps[length - CONV + 1 :].reshape(CONV - 1, map_width),
            ],
            axis=1,
        ),
        "ctx",
        1,
    )
    lead_input = lead_both[:, :inner_width]
    lead_maps = lead_both[:, inner_width:].reshape((CONV - 1,) + state_maps.shape[1:])
    conv_out = causal_conv(ssm_input, lead_input, conv_weight, conv_bias)
    maps_out = causal_conv(state_maps, lead_maps, map_conv, map_bias)
    log_decay = -decay_rate[None, :] * step_size
    running = jnp.cumsum(log_decay.reshape(blocks, BLOCK, head_count), axis=1)
    values = conv_out.reshape(blocks, BLOCK, head_count, HEAD_DIM)
    input_maps = maps_out[:, 0].reshape(blocks, BLOCK, groups, STATE)
    output_maps = maps_out[:, 1].reshape(blocks, BLOCK, groups, STATE)
    block_steps = step_size.reshape(blocks, BLOCK, head_count)
    scores = jnp.einsum(
        "cqgn,csgn->cgqs", output_maps, input_maps, preferred_element_type=jnp.float32
    )
    scores = jnp.broadcast_to(scores[:, :, None], (blocks, groups, repeat, BLOCK, BLOCK)).reshape(
        blocks, head_count, BLOCK, BLOCK
    )
    head_major = jnp.transpose(running, (0, 2, 1))
    gap_log = head_major[:, :, :, None] - head_major[:, :, None, :]
    causal_mask = jnp.tril(jnp.ones((BLOCK, BLOCK), dtype=bool))
    decays = jnp.exp(jnp.where(causal_mask[None, None], gap_log, -1e30))
    step_major = jnp.transpose(block_steps, (0, 2, 1))
    weights = (scores * decays * step_major[:, :, None, :]).astype(jnp.bfloat16)
    within = jnp.einsum("chqs,cshp->cqhp", weights, values, preferred_element_type=jnp.float32)
    to_end = jnp.exp(running[:, -1:, :] - running) * block_steps
    input_heads = jnp.broadcast_to(
        input_maps[:, :, :, None], (blocks, BLOCK, groups, repeat, STATE)
    ).reshape(blocks, BLOCK, head_count, STATE)
    loaded = (input_heads.astype(jnp.float32) * to_end[..., None]).astype(jnp.bfloat16)
    fresh_state = jnp.einsum("cshn,cshp->chnp", loaded, values, preferred_element_type=jnp.float32)
    totals = running[:, -1, :]

    empty_state = jnp.zeros((head_count, STATE, HEAD_DIM), jnp.float32)
    local_enter = []
    carry_state = empty_state
    for block in range(blocks):
        local_enter.append(carry_state)
        carry_state = jnp.exp(totals[block])[:, None, None] * carry_state + fresh_state[block]
    local_end = carry_state
    local_enter = jnp.stack(local_enter)
    device_log = jnp.sum(totals, axis=0)
    before_log, incoming = exclusive_scan(device_log, local_end, "ctx")
    prior_log = jnp.cumsum(totals, axis=0) - totals
    entering = jnp.exp(prior_log)[:, :, None, None] * incoming[None] + local_enter
    carried = entering.astype(jnp.bfloat16).reshape(blocks, groups, repeat, STATE, HEAD_DIM)
    before = jnp.einsum(
        "cqgn,cgrnp->cqgrp", output_maps, carried, preferred_element_type=jnp.float32
    )
    before = jnp.exp(running)[..., None] * before.reshape(blocks, BLOCK, head_count, HEAD_DIM)
    output = within + before + skip_gain[None, None, :, None] * values.astype(jnp.float32)
    gated = output.reshape(length, inner_width) * jax.nn.silu(gate_input.astype(jnp.float32))
    grouped = gated.reshape(length, groups, inner_width // groups)
    inverse_rms = lax.rsqrt(jnp.mean(grouped * grouped, axis=2, keepdims=True) + 1e-05)
    normed = ((grouped * inverse_rms).reshape(length, inner_width) * norm_gain[None, :]).astype(
        jnp.bfloat16
    )
    return scattered_sum(normed, out_weight, "tp")


def solution(mesh):
    in_specs = (
        P("ctx", "tp"),
        P("ctx", "tp"),
        P("ctx", None, "tp"),
        P("ctx", "tp"),
        P("tp"),
        P("tp"),
        P(None, "tp"),
        P("tp"),
        P(None, None, "tp"),
        P(None, "tp"),
        P("tp"),
        P("tp", None),
    )
    out_specs = P(("ctx", "tp"), None)
    return jax.shard_map(local, mesh=mesh, in_specs=in_specs, out_specs=out_specs, check_vma=False)
```

```python
import jax
import jax.numpy as jnp
from jax import lax
from jax.sharding import PartitionSpec as P

HEAD_DIM = 64
STATE = 128
CONV = 4
BLOCK = 128


def passed_along(value, axis, steps):
    count = lax.axis_size(axis)
    first, last = (max(0, -steps), min(count, count - steps))
    return lax.ppermute(value, axis, [(source, source + steps) for source in range(first, last)])


def exclusive_scan(log_total, state, axis):
    count = lax.axis_size(axis)
    heads = state.shape[0]
    window_log, window_state = log_total, state
    prior_log = jnp.zeros_like(log_total)
    prior_state = jnp.zeros_like(state)
    distance = 1
    while distance < count:
        pairs = [(source, source + distance) for source in range(count - distance)]
        high = window_log.astype(jnp.bfloat16)
        low = (window_log - high.astype(jnp.float32)).astype(jnp.bfloat16)
        log_rows = jnp.zeros((1,) + state.shape[1:], jnp.bfloat16)
        log_rows = log_rows.at[0, :heads, 0].set(high).at[0, :heads, 1].set(low)
        packed = jnp.concatenate([window_state.astype(jnp.bfloat16), log_rows], axis=0)
        got = lax.ppermute(packed, axis, pairs)
        got_state = got[:heads].astype(jnp.float32)
        got_log = got[heads, :heads, 0].astype(jnp.float32) + got[heads, :heads, 1].astype(jnp.float32)
        prior_state = jnp.exp(prior_log)[:, None, None] * got_state + prior_state
        prior_log = got_log + prior_log
        if 2 * distance < count:
            window_state = jnp.exp(window_log)[:, None, None] * got_state + window_state
            window_log = got_log + window_log
        distance *= 2
    return prior_log, prior_state


def scattered_sum(rows, weight, axis):
    count = lax.axis_size(axis)
    chips = count // 2
    place = lax.axis_index(axis)
    core = place % 2
    chip = place // 2
    length = rows.shape[0]
    share = length // count
    width = weight.shape[1]
    blocks = rows.reshape(chips, 2, share, rows.shape[1])
    sent_rows = lax.dynamic_index_in_dim(blocks, 1 - core, 1, False)
    kept_rows = lax.dynamic_index_in_dim(blocks, core, 1, False)
    sent = jnp.einsum("ysk,kd->ysd", sent_rows, weight, preferred_element_type=jnp.float32)
    swapped = lax.ppermute(
        sent.astype(jnp.bfloat16), axis, [(source, source ^ 1) for source in range(count)]
    )
    kept = lax.optimization_barrier(
        jnp.einsum("ysk,kd->ysd", kept_rows, weight, preferred_element_type=jnp.float32)
    )
    summed = kept + swapped.astype(jnp.float32)
    if chips == 1:
        return summed[0].astype(jnp.bfloat16)
    half = width // 2
    rightward = [(source, (source + 2) % count) for source in range(count)]
    leftward = [(source, (source - 2) % count) for source in range(count)]
    right_acc = lax.dynamic_index_in_dim(summed, (chip - 1) % chips, 0, False)[:, :half]
    left_acc = lax.dynamic_index_in_dim(summed, (chip + 1) % chips, 0, False)[:, half:]
    for step in range(chips - 1):
        got_right = lax.ppermute(right_acc.astype(jnp.bfloat16), axis, rightward)
        got_left = lax.ppermute(left_acc.astype(jnp.bfloat16), axis, leftward)
        right_own = lax.dynamic_index_in_dim(summed, (chip - 2 - step) % chips, 0, False)[:, :half]
        left_own = lax.dynamic_index_in_dim(summed, (chip + 2 + step) % chips, 0, False)[:, half:]
        right_acc = right_own + got_right.astype(jnp.float32)
        left_acc = left_own + got_left.astype(jnp.float32)
    return jnp.concatenate([right_acc, left_acc], axis=1).astype(jnp.bfloat16)


def causal_conv(values, lead_rows, weight, bias_term):
    padded = lax.optimization_barrier(
        jnp.concatenate([lead_rows, values], axis=0).astype(jnp.float32)
    )
    length = values.shape[0]
    accum = jnp.zeros(values.shape, jnp.float32) + bias_term
    for offset in range(weight.shape[0]):
        accum = accum + weight[offset] * padded[offset : offset + length]
    return jax.nn.silu(accum).astype(jnp.bfloat16)


def local(
    ssm_input,
    gate_input,
    state_maps,
    step_size,
    decay_rate,
    skip_gain,
    conv_weight,
    conv_bias,
    map_conv,
    map_bias,
    norm_gain,
    out_weight,
):
    length = ssm_input.shape[0]
    head_count = step_size.shape[1]
    inner_width = ssm_input.shape[1]
    groups = state_maps.shape[2] // STATE
    repeat = head_count // groups
    blocks = length // BLOCK
    map_width = state_maps.shape[1] * state_maps.shape[2]
    lead_both = passed_along(
        jnp.concatenate(
            [
                ssm_input[length - CONV + 1 :],
                state_maps[length - CONV + 1 :].reshape(CONV - 1, map_width),
            ],
            axis=1,
        ),
        "ctx",
        1,
    )
    lead_input = lead_both[:, :inner_width]
    lead_maps = lead_both[:, inner_width:].reshape((CONV - 1,) + state_maps.shape[1:])
    conv_out = causal_conv(ssm_input, lead_input, conv_weight, conv_bias)
    maps_out = causal_conv(state_maps, lead_maps, map_conv, map_bias)
    log_decay = -decay_rate[None, :] * step_size
    running = jnp.cumsum(log_decay.reshape(blocks, BLOCK, head_count), axis=1)
    values = conv_out.reshape(blocks, BLOCK, head_count, HEAD_DIM)
    input_maps = maps_out[:, 0].reshape(blocks, BLOCK, groups, STATE)
    output_maps = maps_out[:, 1].reshape(blocks, BLOCK, groups, STATE)
    block_steps = step_size.reshape(blocks, BLOCK, head_count)
    scores = jnp.einsum(
        "cqgn,csgn->cgqs", output_maps, input_maps, preferred_element_type=jnp.float32
    )
    scores = jnp.broadcast_to(scores[:, :, None], (blocks, groups, repeat, BLOCK, BLOCK)).reshape(
        blocks, head_count, BLOCK, BLOCK
    )
    head_major = jnp.transpose(running, (0, 2, 1))
    gap_log = head_major[:, :, :, None] - head_major[:, :, None, :]
    causal_mask = jnp.tril(jnp.ones((BLOCK, BLOCK), dtype=bool))
    decays = jnp.exp(jnp.where(causal_mask[None, None], gap_log, -1e30))
    step_major = jnp.transpose(block_steps, (0, 2, 1))
    weights = (scores * decays * step_major[:, :, None, :]).astype(jnp.bfloat16)
    within = jnp.einsum("chqs,cshp->cqhp", weights, values, preferred_element_type=jnp.float32)
    to_end = jnp.exp(running[:, -1:, :] - running) * block_steps
    input_heads = jnp.broadcast_to(
        input_maps[:, :, :, None], (blocks, BLOCK, groups, repeat, STATE)
    ).reshape(blocks, BLOCK, head_count, STATE)
    loaded = (input_heads.astype(jnp.float32) * to_end[..., None]).astype(jnp.bfloat16)
    fresh_state = jnp.einsum("cshn,cshp->chnp", loaded, values, preferred_element_type=jnp.float32)
    totals = running[:, -1, :]

    empty_state = jnp.zeros((head_count, STATE, HEAD_DIM), jnp.float32)
    local_enter = []
    carry_state = empty_state
    for block in range(blocks):
        local_enter.append(carry_state)
        carry_state = jnp.exp(totals[block])[:, None, None] * carry_state + fresh_state[block]
    local_end = carry_state
    local_enter = jnp.stack(local_enter)
    device_log = jnp.sum(totals, axis=0)
    before_log, incoming = exclusive_scan(device_log, local_end, "ctx")
    prior_log = jnp.cumsum(totals, axis=0) - totals
    entering = jnp.exp(prior_log)[:, :, None, None] * incoming[None] + local_enter
    carried = (
        entering.reshape(blocks, groups, repeat, STATE, HEAD_DIM)
        .transpose(0, 1, 3, 2, 4)
        .reshape(blocks, groups, STATE, repeat * HEAD_DIM)
        .astype(jnp.bfloat16)
    )
    before = jnp.einsum(
        "cqgn,cgnk->cqgk", output_maps, carried, preferred_element_type=jnp.float32
    ).reshape(length, inner_width)
    lane_scale = jnp.broadcast_to(
        jnp.exp(running)[..., None], (blocks, BLOCK, head_count, HEAD_DIM)
    ).reshape(length, inner_width)
    skip_lanes = jnp.broadcast_to(skip_gain[:, None], (head_count, HEAD_DIM)).reshape(inner_width)
    output = (
        within.reshape(length, inner_width)
        + lane_scale * before
        + skip_lanes[None, :] * conv_out.astype(jnp.float32)
    )
    gated = output * jax.nn.silu(gate_input.astype(jnp.float32))
    grouped = gated.reshape(length, groups, inner_width // groups)
    inverse_rms = lax.rsqrt(jnp.mean(grouped * grouped, axis=2, keepdims=True) + 1e-05)
    normed = ((grouped * inverse_rms).reshape(length, inner_width) * norm_gain[None, :]).astype(
        jnp.bfloat16
    )
    return scattered_sum(normed, out_weight, "tp")


def solution(mesh):
    in_specs = (
        P("ctx", "tp"),
        P("ctx", "tp"),
        P("ctx", None, "tp"),
        P("ctx", "tp"),
        P("tp"),
        P("tp"),
        P(None, "tp"),
        P("tp"),
        P(None, None, "tp"),
        P(None, "tp"),
        P("tp"),
        P("tp", None),
    )
    out_specs = P(("ctx", "tp"), None)
    return jax.shard_map(local, mesh=mesh, in_specs=in_specs, out_specs=out_specs, check_vma=False)
```

```python
import jax
import jax.numpy as jnp
from jax import lax
from jax.sharding import PartitionSpec as P

HEAD_DIM = 64
STATE = 128
CONV = 4
BLOCK = 128


def passed_along(value, axis, steps):
    count = lax.axis_size(axis)
    first, last = (max(0, -steps), min(count, count - steps))
    return lax.ppermute(value, axis, [(source, source + steps) for source in range(first, last)])


def exclusive_scan(log_total, state, axis):
    count = lax.axis_size(axis)
    window_log, window_state = log_total, state
    prior_log = jnp.zeros_like(log_total)
    prior_state = jnp.zeros_like(state)
    distance = 1
    while distance < count:
        pairs = [(source, source + distance) for source in range(count - distance)]
        got_log = lax.ppermute(window_log, axis, pairs)
        got_state = lax.ppermute(window_state.astype(jnp.bfloat16), axis, pairs).astype(jnp.float32)
        prior_state = jnp.exp(prior_log)[:, None, None] * got_state + prior_state
        prior_log = got_log + prior_log
        if 2 * distance < count:
            window_state = jnp.exp(window_log)[:, None, None] * got_state + window_state
            window_log = got_log + window_log
        distance *= 2
    return prior_log, prior_state


def scattered_sum(rows, weight, axis):
    count = lax.axis_size(axis)
    chips = count // 2
    place = lax.axis_index(axis)
    core = place % 2
    chip = place // 2
    length = rows.shape[0]
    share = length // count
    width = weight.shape[1]
    blocks = rows.reshape(chips, 2, share, rows.shape[1])
    sent_rows = lax.dynamic_index_in_dim(blocks, 1 - core, 1, False)
    kept_rows = lax.dynamic_index_in_dim(blocks, core, 1, False)
    sent = jnp.einsum("ysk,kd->ysd", sent_rows, weight, preferred_element_type=jnp.float32)
    swapped = lax.ppermute(
        sent.astype(jnp.bfloat16), axis, [(source, source ^ 1) for source in range(count)]
    )
    kept = lax.optimization_barrier(
        jnp.einsum("ysk,kd->ysd", kept_rows, weight, preferred_element_type=jnp.float32)
    )
    summed = kept + swapped.astype(jnp.float32)
    if chips == 1:
        return summed[0].astype(jnp.bfloat16)
    half = width // 2
    rightward = [(source, (source + 2) % count) for source in range(count)]
    leftward = [(source, (source - 2) % count) for source in range(count)]
    right_acc = lax.dynamic_index_in_dim(summed, (chip - 1) % chips, 0, False)[:, :half]
    left_acc = lax.dynamic_index_in_dim(summed, (chip + 1) % chips, 0, False)[:, half:]
    for step in range(chips - 1):
        got_right = lax.ppermute(right_acc.astype(jnp.bfloat16), axis, rightward)
        got_left = lax.ppermute(left_acc.astype(jnp.bfloat16), axis, leftward)
        right_own = lax.dynamic_index_in_dim(summed, (chip - 2 - step) % chips, 0, False)[:, :half]
        left_own = lax.dynamic_index_in_dim(summed, (chip + 2 + step) % chips, 0, False)[:, half:]
        right_acc = right_own + got_right.astype(jnp.float32)
        left_acc = left_own + got_left.astype(jnp.float32)
    return jnp.concatenate([right_acc, left_acc], axis=1).astype(jnp.bfloat16)


def causal_conv(values, lead_rows, weight, bias_term):
    padded = lax.optimization_barrier(
        jnp.concatenate([lead_rows, values], axis=0).astype(jnp.float32)
    )
    length = values.shape[0]
    accum = jnp.zeros(values.shape, jnp.float32) + bias_term
    for offset in range(weight.shape[0]):
        accum = accum + weight[offset] * padded[offset : offset + length]
    return jax.nn.silu(accum).astype(jnp.bfloat16)


def local(
    ssm_input,
    gate_input,
    state_maps,
    step_size,
    decay_rate,
    skip_gain,
    conv_weight,
    conv_bias,
    map_conv,
    map_bias,
    norm_gain,
    out_weight,
):
    length = ssm_input.shape[0]
    head_count = step_size.shape[1]
    inner_width = ssm_input.shape[1]
    groups = state_maps.shape[2] // STATE
    repeat = head_count // groups
    blocks = length // BLOCK
    map_width = state_maps.shape[1] * state_maps.shape[2]
    lead_both = passed_along(
        jnp.concatenate(
            [
                ssm_input[length - CONV + 1 :],
                state_maps[length - CONV + 1 :].reshape(CONV - 1, map_width),
            ],
            axis=1,
        ),
        "ctx",
        1,
    )
    lead_input = lead_both[:, :inner_width]
    lead_maps = lead_both[:, inner_width:].reshape((CONV - 1,) + state_maps.shape[1:])
    conv_out = causal_conv(ssm_input, lead_input, conv_weight, conv_bias)
    maps_out = causal_conv(state_maps, lead_maps, map_conv, map_bias)
    log_decay = -decay_rate[None, :] * step_size
    running = jnp.cumsum(log_decay.reshape(blocks, BLOCK, head_count), axis=1)
    values = conv_out.reshape(blocks, BLOCK, head_count, HEAD_DIM)
    input_maps = maps_out[:, 0].reshape(blocks, BLOCK, groups, STATE)
    output_maps = maps_out[:, 1].reshape(blocks, BLOCK, groups, STATE)
    block_steps = step_size.reshape(blocks, BLOCK, head_count)
    scores = jnp.einsum(
        "cqgn,csgn->cgqs", output_maps, input_maps, preferred_element_type=jnp.float32
    )
    scores = jnp.broadcast_to(scores[:, :, None], (blocks, groups, repeat, BLOCK, BLOCK)).reshape(
        blocks, head_count, BLOCK, BLOCK
    )
    head_major = jnp.transpose(running, (0, 2, 1))
    gap_log = head_major[:, :, :, None] - head_major[:, :, None, :]
    causal_mask = jnp.tril(jnp.ones((BLOCK, BLOCK), dtype=bool))
    decays = jnp.exp(jnp.where(causal_mask[None, None], gap_log, -1e30))
    step_major = jnp.transpose(block_steps, (0, 2, 1))
    weights = (scores * decays * step_major[:, :, None, :]).astype(jnp.bfloat16)
    within = jnp.einsum("chqs,cshp->cqhp", weights, values, preferred_element_type=jnp.float32)
    to_end = jnp.exp(running[:, -1:, :] - running) * block_steps
    input_heads = jnp.broadcast_to(
        input_maps[:, :, :, None], (blocks, BLOCK, groups, repeat, STATE)
    ).reshape(blocks, BLOCK, head_count, STATE)
    loaded = (input_heads.astype(jnp.float32) * to_end[..., None]).astype(jnp.bfloat16)
    fresh_state = jnp.einsum("cshn,cshp->chnp", loaded, values, preferred_element_type=jnp.float32)
    totals = running[:, -1, :]

    empty_state = jnp.zeros((head_count, STATE, HEAD_DIM), jnp.float32)
    local_enter = []
    carry_state = empty_state
    for block in range(blocks):
        local_enter.append(carry_state)
        carry_state = jnp.exp(totals[block])[:, None, None] * carry_state + fresh_state[block]
    local_end = carry_state
    local_enter = jnp.stack(local_enter)
    device_log = jnp.sum(totals, axis=0)
    before_log, incoming = exclusive_scan(device_log, local_end, "ctx")
    prior_log = jnp.cumsum(totals, axis=0) - totals
    entering = jnp.exp(prior_log)[:, :, None, None] * incoming[None] + local_enter
    carried = entering.astype(jnp.bfloat16).reshape(blocks, groups, repeat, STATE, HEAD_DIM)
    before = jnp.einsum(
        "cqgn,cgrnp->cqgrp", output_maps, carried, preferred_element_type=jnp.float32
    )
    before = jnp.exp(running)[..., None] * before.reshape(blocks, BLOCK, head_count, HEAD_DIM)
    output = within + before + skip_gain[None, None, :, None] * values.astype(jnp.float32)
    gated = output.reshape(length, inner_width) * jax.nn.silu(gate_input.astype(jnp.float32))
    grouped = gated.reshape(length, groups, inner_width // groups)
    inverse_rms = lax.rsqrt(jnp.mean(grouped * grouped, axis=2, keepdims=True) + 1e-05)
    normed = ((grouped * inverse_rms).reshape(length, inner_width) * norm_gain[None, :]).astype(
        jnp.bfloat16
    )
    return scattered_sum(normed, out_weight, "tp")


def solution(mesh):
    in_specs = (
        P("ctx", "tp"),
        P("ctx", "tp"),
        P("ctx", None, "tp"),
        P("ctx", "tp"),
        P("tp"),
        P("tp"),
        P(None, "tp"),
        P("tp"),
        P(None, None, "tp"),
        P(None, "tp"),
        P("tp"),
        P("tp", None),
    )
    out_specs = P(("ctx", "tp"), None)
    return jax.shard_map(local, mesh=mesh, in_specs=in_specs, out_specs=out_specs, check_vma=False)
```

```python
import jax
import jax.numpy as jnp
from jax import lax
from jax.sharding import PartitionSpec as P

HEAD_DIM = 64
STATE = 128
CONV = 4
BLOCK = 128


def passed_along(value, axis, steps):
    count = lax.axis_size(axis)
    first, last = (max(0, -steps), min(count, count - steps))
    return lax.ppermute(value, axis, [(source, source + steps) for source in range(first, last)])


def exclusive_scan(log_total, state, axis):
    count = lax.axis_size(axis)
    heads = state.shape[0]
    rows, cols = state.shape[1:]
    window_log, window_state = log_total, state
    prior_log = jnp.zeros_like(log_total)
    prior_state = jnp.zeros_like(state)
    distance = 1
    while distance < count:
        pairs = [(source, source + distance) for source in range(count - distance)]
        high = window_log.astype(jnp.bfloat16)
        low = (window_log - high.astype(jnp.float32)).astype(jnp.bfloat16)
        log_rows = jnp.pad(jnp.stack([high, low], axis=1), ((0, rows - heads), (0, cols - 2)))
        packed = jnp.concatenate([window_state.astype(jnp.bfloat16), log_rows[None]], axis=0)
        got = lax.ppermute(packed, axis, pairs)
        got_state = got[:heads].astype(jnp.float32)
        got_log = got[heads, :heads, 0].astype(jnp.float32) + got[heads, :heads, 1].astype(jnp.float32)
        prior_state = jnp.exp(prior_log)[:, None, None] * got_state + prior_state
        prior_log = got_log + prior_log
        if 2 * distance < count:
            window_state = jnp.exp(window_log)[:, None, None] * got_state + window_state
            window_log = got_log + window_log
        distance *= 2
    return prior_log, prior_state


def scattered_sum(rows, weight, axis):
    count = lax.axis_size(axis)
    chips = count // 2
    place = lax.axis_index(axis)
    core = place % 2
    chip = place // 2
    length = rows.shape[0]
    share = length // count
    width = weight.shape[1]
    blocks = rows.reshape(chips, 2, share, rows.shape[1])
    sent_rows = lax.dynamic_index_in_dim(blocks, 1 - core, 1, False)
    kept_rows = lax.dynamic_index_in_dim(blocks, core, 1, False)
    sent = jnp.einsum("ysk,kd->ysd", sent_rows, weight, preferred_element_type=jnp.float32)
    swapped = lax.ppermute(
        sent.astype(jnp.bfloat16), axis, [(source, source ^ 1) for source in range(count)]
    )
    kept = lax.optimization_barrier(
        jnp.einsum("ysk,kd->ysd", kept_rows, weight, preferred_element_type=jnp.float32)
    )
    summed = kept + swapped.astype(jnp.float32)
    if chips == 1:
        return summed[0].astype(jnp.bfloat16)
    half = width // 2
    rightward = [(source, (source + 2) % count) for source in range(count)]
    leftward = [(source, (source - 2) % count) for source in range(count)]
    right_acc = lax.dynamic_index_in_dim(summed, (chip - 1) % chips, 0, False)[:, :half]
    left_acc = lax.dynamic_index_in_dim(summed, (chip + 1) % chips, 0, False)[:, half:]
    for step in range(chips - 1):
        got_right = lax.ppermute(right_acc.astype(jnp.bfloat16), axis, rightward)
        got_left = lax.ppermute(left_acc.astype(jnp.bfloat16), axis, leftward)
        right_own = lax.dynamic_index_in_dim(summed, (chip - 2 - step) % chips, 0, False)[:, :half]
        left_own = lax.dynamic_index_in_dim(summed, (chip + 2 + step) % chips, 0, False)[:, half:]
        right_acc = right_own + got_right.astype(jnp.float32)
        left_acc = left_own + got_left.astype(jnp.float32)
    return jnp.concatenate([right_acc, left_acc], axis=1).astype(jnp.bfloat16)


def causal_conv(values, lead_rows, weight, bias_term):
    padded = lax.optimization_barrier(
        jnp.concatenate([lead_rows, values], axis=0).astype(jnp.float32)
    )
    length = values.shape[0]
    accum = jnp.zeros(values.shape, jnp.float32) + bias_term
    for offset in range(weight.shape[0]):
        accum = accum + weight[offset] * padded[offset : offset + length]
    return jax.nn.silu(accum).astype(jnp.bfloat16)


def local(
    ssm_input,
    gate_input,
    state_maps,
    step_size,
    decay_rate,
    skip_gain,
    conv_weight,
    conv_bias,
    map_conv,
    map_bias,
    norm_gain,
    out_weight,
):
    length = ssm_input.shape[0]
    head_count = step_size.shape[1]
    inner_width = ssm_input.shape[1]
    groups = state_maps.shape[2] // STATE
    repeat = head_count // groups
    blocks = length // BLOCK
    map_width = state_maps.shape[1] * state_maps.shape[2]
    lead_both = passed_along(
        jnp.concatenate(
            [
                ssm_input[length - CONV + 1 :],
                state_maps[length - CONV + 1 :].reshape(CONV - 1, map_width),
            ],
            axis=1,
        ),
        "ctx",
        1,
    )
    lead_input = lead_both[:, :inner_width]
    lead_maps = lead_both[:, inner_width:].reshape((CONV - 1,) + state_maps.shape[1:])
    conv_out = causal_conv(ssm_input, lead_input, conv_weight, conv_bias)
    maps_out = causal_conv(state_maps, lead_maps, map_conv, map_bias)
    log_decay = -decay_rate[None, :] * step_size
    running = jnp.cumsum(log_decay.reshape(blocks, BLOCK, head_count), axis=1)
    values = conv_out.reshape(blocks, BLOCK, head_count, HEAD_DIM)
    input_maps = maps_out[:, 0].reshape(blocks, BLOCK, groups, STATE)
    output_maps = maps_out[:, 1].reshape(blocks, BLOCK, groups, STATE)
    block_steps = step_size.reshape(blocks, BLOCK, head_count)
    scores = jnp.einsum(
        "cqgn,csgn->cgqs", output_maps, input_maps, preferred_element_type=jnp.float32
    )
    scores = jnp.broadcast_to(scores[:, :, None], (blocks, groups, repeat, BLOCK, BLOCK)).reshape(
        blocks, head_count, BLOCK, BLOCK
    )
    head_major = jnp.transpose(running, (0, 2, 1))
    gap_log = head_major[:, :, :, None] - head_major[:, :, None, :]
    causal_mask = jnp.tril(jnp.ones((BLOCK, BLOCK), dtype=bool))
    decays = jnp.exp(jnp.where(causal_mask[None, None], gap_log, -1e30))
    step_major = jnp.transpose(block_steps, (0, 2, 1))
    weights = (scores * decays * step_major[:, :, None, :]).astype(jnp.bfloat16)
    within = jnp.einsum("chqs,cshp->cqhp", weights, values, preferred_element_type=jnp.float32)
    to_end = jnp.exp(running[:, -1:, :] - running) * block_steps
    input_heads = jnp.broadcast_to(
        input_maps[:, :, :, None], (blocks, BLOCK, groups, repeat, STATE)
    ).reshape(blocks, BLOCK, head_count, STATE)
    loaded = (input_heads.astype(jnp.float32) * to_end[..., None]).astype(jnp.bfloat16)
    fresh_state = jnp.einsum("cshn,cshp->chnp", loaded, values, preferred_element_type=jnp.float32)
    totals = running[:, -1, :]

    empty_state = jnp.zeros((head_count, STATE, HEAD_DIM), jnp.float32)
    local_enter = []
    carry_state = empty_state
    for block in range(blocks):
        local_enter.append(carry_state)
        carry_state = jnp.exp(totals[block])[:, None, None] * carry_state + fresh_state[block]
    local_end = carry_state
    local_enter = jnp.stack(local_enter)
    device_log = jnp.sum(totals, axis=0)
    before_log, incoming = exclusive_scan(device_log, local_end, "ctx")
    prior_log = jnp.cumsum(totals, axis=0) - totals
    entering = jnp.exp(prior_log)[:, :, None, None] * incoming[None] + local_enter
    carried = entering.astype(jnp.bfloat16).reshape(blocks, groups, repeat, STATE, HEAD_DIM)
    before = jnp.einsum(
        "cqgn,cgrnp->cqgrp", output_maps, carried, preferred_element_type=jnp.float32
    )
    before = jnp.exp(running)[..., None] * before.reshape(blocks, BLOCK, head_count, HEAD_DIM)
    output = within + before + skip_gain[None, None, :, None] * values.astype(jnp.float32)
    gated = output.reshape(length, inner_width) * jax.nn.silu(gate_input.astype(jnp.float32))
    grouped = gated.reshape(length, groups, inner_width // groups)
    inverse_rms = lax.rsqrt(jnp.mean(grouped * grouped, axis=2, keepdims=True) + 1e-05)
    normed = ((grouped * inverse_rms).reshape(length, inner_width) * norm_gain[None, :]).astype(
        jnp.bfloat16
    )
    return scattered_sum(normed, out_weight, "tp")


def solution(mesh):
    in_specs = (
        P("ctx", "tp"),
        P("ctx", "tp"),
        P("ctx", None, "tp"),
        P("ctx", "tp"),
        P("tp"),
        P("tp"),
        P(None, "tp"),
        P("tp"),
        P(None, None, "tp"),
        P(None, "tp"),
        P("tp"),
        P("tp", None),
    )
    out_specs = P(("ctx", "tp"), None)
    return jax.shard_map(local, mesh=mesh, in_specs=in_specs, out_specs=out_specs, check_vma=False)
```

```python
import jax
import jax.numpy as jnp
from jax import lax
from jax.sharding import PartitionSpec as P

HEAD_DIM = 64
STATE = 128
CONV = 4
BLOCK = 128


def passed_along(value, axis, steps):
    count = lax.axis_size(axis)
    first, last = (max(0, -steps), min(count, count - steps))
    return lax.ppermute(value, axis, [(source, source + steps) for source in range(first, last)])


def exclusive_scan(log_total, state, axis):
    count = lax.axis_size(axis)
    heads = state.shape[0]
    rows, cols = state.shape[1:]
    window_log, window_state = log_total, state
    prior_log = jnp.zeros_like(log_total)
    prior_state = jnp.zeros_like(state)
    distance = 1
    while distance < count:
        pairs = [(source, source + distance) for source in range(count - distance)]
        high = window_log.astype(jnp.bfloat16)
        low = (window_log - high.astype(jnp.float32)).astype(jnp.bfloat16)
        log_rows = jnp.pad(jnp.stack([high, low], axis=1), ((0, rows - heads), (0, cols - 2)))
        packed = jnp.concatenate([window_state.astype(jnp.bfloat16), log_rows[None]], axis=0)
        got = lax.ppermute(packed, axis, pairs)
        got_state = got[:heads].astype(jnp.float32)
        got_log = got[heads, :heads, 0].astype(jnp.float32) + got[heads, :heads, 1].astype(jnp.float32)
        prior_state = jnp.exp(prior_log)[:, None, None] * got_state + prior_state
        prior_log = got_log + prior_log
        if 2 * distance < count:
            window_state = jnp.exp(window_log)[:, None, None] * got_state + window_state
            window_log = got_log + window_log
        distance *= 2
    return prior_log, prior_state


def scattered_sum(rows, weight, axis):
    count = lax.axis_size(axis)
    chips = count // 2
    place = lax.axis_index(axis)
    core = place % 2
    chip = place // 2
    length = rows.shape[0]
    share = length // count
    width = weight.shape[1]
    blocks = rows.reshape(chips, 2, share, rows.shape[1])
    sent_rows = lax.dynamic_index_in_dim(blocks, 1 - core, 1, False)
    kept_rows = lax.dynamic_index_in_dim(blocks, core, 1, False)
    sent = jnp.einsum("ysk,kd->ysd", sent_rows, weight, preferred_element_type=jnp.float32)
    swapped = lax.ppermute(
        sent.astype(jnp.bfloat16), axis, [(source, source ^ 1) for source in range(count)]
    )
    kept = lax.optimization_barrier(
        jnp.einsum("ysk,kd->ysd", kept_rows, weight, preferred_element_type=jnp.float32)
    )
    summed = kept + swapped.astype(jnp.float32)
    if chips == 1:
        return summed[0].astype(jnp.bfloat16)
    half = width // 2
    rightward = [(source, (source + 2) % count) for source in range(count)]
    leftward = [(source, (source - 2) % count) for source in range(count)]
    right_acc = lax.dynamic_index_in_dim(summed, (chip - 1) % chips, 0, False)[:, :half]
    left_acc = lax.dynamic_index_in_dim(summed, (chip + 1) % chips, 0, False)[:, half:]
    for step in range(chips - 1):
        got_right = lax.ppermute(right_acc.astype(jnp.bfloat16), axis, rightward)
        got_left = lax.ppermute(left_acc.astype(jnp.bfloat16), axis, leftward)
        right_own = lax.dynamic_index_in_dim(summed, (chip - 2 - step) % chips, 0, False)[:, :half]
        left_own = lax.dynamic_index_in_dim(summed, (chip + 2 + step) % chips, 0, False)[:, half:]
        right_acc = right_own + got_right.astype(jnp.float32)
        left_acc = left_own + got_left.astype(jnp.float32)
    return jnp.concatenate([right_acc, left_acc], axis=1).astype(jnp.bfloat16)


def causal_conv(values, lead_rows, weight, bias_term):
    padded = lax.optimization_barrier(
        jnp.concatenate([lead_rows, values], axis=0).astype(jnp.float32)
    )
    length = values.shape[0]
    accum = jnp.zeros(values.shape, jnp.float32) + bias_term
    for offset in range(weight.shape[0]):
        accum = accum + weight[offset] * padded[offset : offset + length]
    return jax.nn.silu(accum).astype(jnp.bfloat16)


def local(
    ssm_input,
    gate_input,
    state_maps,
    step_size,
    decay_rate,
    skip_gain,
    conv_weight,
    conv_bias,
    map_conv,
    map_bias,
    norm_gain,
    out_weight,
):
    length = ssm_input.shape[0]
    head_count = step_size.shape[1]
    inner_width = ssm_input.shape[1]
    groups = state_maps.shape[2] // STATE
    repeat = head_count // groups
    blocks = length // BLOCK
    map_width = state_maps.shape[1] * state_maps.shape[2]
    lead_both = passed_along(
        jnp.concatenate(
            [
                ssm_input[length - CONV + 1 :],
                state_maps[length - CONV + 1 :].reshape(CONV - 1, map_width),
            ],
            axis=1,
        ),
        "ctx",
        1,
    )
    lead_input = lead_both[:, :inner_width]
    lead_maps = lead_both[:, inner_width:].reshape((CONV - 1,) + state_maps.shape[1:])
    conv_out = causal_conv(ssm_input, lead_input, conv_weight, conv_bias)
    maps_out = causal_conv(state_maps, lead_maps, map_conv, map_bias)
    log_decay = -decay_rate[None, :] * step_size
    running = jnp.cumsum(log_decay.reshape(blocks, BLOCK, head_count), axis=1)
    values = conv_out.reshape(blocks, BLOCK, head_count, HEAD_DIM)
    input_maps = maps_out[:, 0].reshape(blocks, BLOCK, groups, STATE)
    output_maps = maps_out[:, 1].reshape(blocks, BLOCK, groups, STATE)
    block_steps = step_size.reshape(blocks, BLOCK, head_count)
    scores = jnp.einsum(
        "cqgn,csgn->cgqs", output_maps, input_maps, preferred_element_type=jnp.float32
    )
    scores = jnp.broadcast_to(scores[:, :, None], (blocks, groups, repeat, BLOCK, BLOCK)).reshape(
        blocks, head_count, BLOCK, BLOCK
    )
    head_major = jnp.transpose(running, (0, 2, 1))
    gap_log = head_major[:, :, :, None] - head_major[:, :, None, :]
    causal_mask = jnp.tril(jnp.ones((BLOCK, BLOCK), dtype=bool))
    decays = jnp.exp(jnp.where(causal_mask[None, None], gap_log, -1e30))
    step_major = jnp.transpose(block_steps, (0, 2, 1))
    weights = (scores * decays * step_major[:, :, None, :]).astype(jnp.bfloat16)
    within = jnp.einsum("chqs,cshp->cqhp", weights, values, preferred_element_type=jnp.float32)
    to_end = jnp.exp(running[:, -1:, :] - running) * block_steps
    input_heads = jnp.broadcast_to(
        input_maps[:, :, :, None], (blocks, BLOCK, groups, repeat, STATE)
    ).reshape(blocks, BLOCK, head_count, STATE)
    loaded = (input_heads.astype(jnp.float32) * to_end[..., None]).astype(jnp.bfloat16)
    fresh_state = jnp.einsum("cshn,cshp->chnp", loaded, values, preferred_element_type=jnp.float32)
    totals = running[:, -1, :]

    empty_state = jnp.zeros((head_count, STATE, HEAD_DIM), jnp.float32)
    local_enter = []
    carry_state = empty_state
    for block in range(blocks):
        local_enter.append(carry_state)
        carry_state = jnp.exp(totals[block])[:, None, None] * carry_state + fresh_state[block]
    local_end = carry_state
    local_enter = jnp.stack(local_enter)
    device_log = jnp.sum(totals, axis=0)
    before_log, incoming = exclusive_scan(device_log, local_end, "ctx")
    prior_log = jnp.cumsum(totals, axis=0) - totals
    entering = jnp.exp(prior_log)[:, :, None, None] * incoming[None] + local_enter
    carried = entering.astype(jnp.bfloat16).reshape(blocks, groups, repeat, STATE, HEAD_DIM)
    before = jnp.einsum(
        "cqgn,cgrnp->cqgrp", output_maps, carried, preferred_element_type=jnp.float32
    )
    before = jnp.exp(running)[..., None] * before.reshape(blocks, BLOCK, head_count, HEAD_DIM)
    output = within + before + skip_gain[None, None, :, None] * values.astype(jnp.float32)
    gated = output.reshape(length, inner_width) * jax.nn.silu(gate_input.astype(jnp.float32))
    grouped = gated.reshape(length, groups, inner_width // groups)
    inverse_rms = lax.rsqrt(jnp.mean(grouped * grouped, axis=2, keepdims=True) + 1e-05)
    normed = lax.optimization_barrier(
        ((grouped * inverse_rms).reshape(length, inner_width) * norm_gain[None, :]).astype(
            jnp.bfloat16
        )
    )
    return scattered_sum(normed, out_weight, "tp")


def solution(mesh):
    in_specs = (
        P("ctx", "tp"),
        P("ctx", "tp"),
        P("ctx", None, "tp"),
        P("ctx", "tp"),
        P("tp"),
        P("tp"),
        P(None, "tp"),
        P("tp"),
        P(None, None, "tp"),
        P(None, "tp"),
        P("tp"),
        P("tp", None),
    )
    out_specs = P(("ctx", "tp"), None)
    return jax.shard_map(local, mesh=mesh, in_specs=in_specs, out_specs=out_specs, check_vma=False)
```

```python
import jax
import jax.numpy as jnp
from jax import lax
from jax.experimental.layout import Layout, with_layout_constraint
from jax.sharding import PartitionSpec as P

HEAD_DIM = 64
STATE = 128
CONV = 4
BLOCK = 128


def passed_along(value, axis, steps):
    count = lax.axis_size(axis)
    first, last = (max(0, -steps), min(count, count - steps))
    return lax.ppermute(value, axis, [(source, source + steps) for source in range(first, last)])


def exclusive_scan(log_total, state, axis):
    count = lax.axis_size(axis)
    heads = state.shape[0]
    rows, cols = state.shape[1:]
    window_log, window_state = log_total, state
    prior_log = jnp.zeros_like(log_total)
    prior_state = jnp.zeros_like(state)
    distance = 1
    while distance < count:
        pairs = [(source, source + distance) for source in range(count - distance)]
        high = window_log.astype(jnp.bfloat16)
        low = (window_log - high.astype(jnp.float32)).astype(jnp.bfloat16)
        log_rows = jnp.pad(jnp.stack([high, low], axis=1), ((0, rows - heads), (0, cols - 2)))
        packed = jnp.concatenate([window_state.astype(jnp.bfloat16), log_rows[None]], axis=0)
        got = lax.ppermute(packed, axis, pairs)
        got_state = got[:heads].astype(jnp.float32)
        got_log = got[heads, :heads, 0].astype(jnp.float32) + got[heads, :heads, 1].astype(jnp.float32)
        prior_state = jnp.exp(prior_log)[:, None, None] * got_state + prior_state
        prior_log = got_log + prior_log
        if 2 * distance < count:
            window_state = jnp.exp(window_log)[:, None, None] * got_state + window_state
            window_log = got_log + window_log
        distance *= 2
    return prior_log, prior_state


def scattered_sum(rows, weight, axis):
    count = lax.axis_size(axis)
    chips = count // 2
    place = lax.axis_index(axis)
    core = place % 2
    chip = place // 2
    length = rows.shape[0]
    share = length // count
    width = weight.shape[1]
    blocks = rows.reshape(chips, 2, share, rows.shape[1])
    sent_rows = lax.dynamic_index_in_dim(blocks, 1 - core, 1, False)
    kept_rows = lax.dynamic_index_in_dim(blocks, core, 1, False)
    sent = jnp.einsum("ysk,kd->ysd", sent_rows, weight, preferred_element_type=jnp.float32)
    swapped = lax.ppermute(
        sent.astype(jnp.bfloat16), axis, [(source, source ^ 1) for source in range(count)]
    )
    kept = lax.optimization_barrier(
        jnp.einsum("ysk,kd->ysd", kept_rows, weight, preferred_element_type=jnp.float32)
    )
    summed = kept + swapped.astype(jnp.float32)
    if chips == 1:
        return summed[0].astype(jnp.bfloat16)
    half = width // 2
    rightward = [(source, (source + 2) % count) for source in range(count)]
    leftward = [(source, (source - 2) % count) for source in range(count)]
    right_acc = lax.dynamic_index_in_dim(summed, (chip - 1) % chips, 0, False)[:, :half]
    left_acc = lax.dynamic_index_in_dim(summed, (chip + 1) % chips, 0, False)[:, half:]
    for step in range(chips - 1):
        got_right = lax.ppermute(right_acc.astype(jnp.bfloat16), axis, rightward)
        got_left = lax.ppermute(left_acc.astype(jnp.bfloat16), axis, leftward)
        right_own = lax.dynamic_index_in_dim(summed, (chip - 2 - step) % chips, 0, False)[:, :half]
        left_own = lax.dynamic_index_in_dim(summed, (chip + 2 + step) % chips, 0, False)[:, half:]
        right_acc = right_own + got_right.astype(jnp.float32)
        left_acc = left_own + got_left.astype(jnp.float32)
    return jnp.concatenate([right_acc, left_acc], axis=1).astype(jnp.bfloat16)


def causal_conv(values, lead_rows, weight, bias_term):
    padded = lax.optimization_barrier(
        jnp.concatenate([lead_rows, values], axis=0).astype(jnp.float32)
    )
    length = values.shape[0]
    accum = jnp.zeros(values.shape, jnp.float32) + bias_term
    for offset in range(weight.shape[0]):
        accum = accum + weight[offset] * padded[offset : offset + length]
    return jax.nn.silu(accum).astype(jnp.bfloat16)


def local(
    ssm_input,
    gate_input,
    state_maps,
    step_size,
    decay_rate,
    skip_gain,
    conv_weight,
    conv_bias,
    map_conv,
    map_bias,
    norm_gain,
    out_weight,
):
    length = ssm_input.shape[0]
    head_count = step_size.shape[1]
    inner_width = ssm_input.shape[1]
    groups = state_maps.shape[2] // STATE
    repeat = head_count // groups
    blocks = length // BLOCK
    map_width = state_maps.shape[1] * state_maps.shape[2]
    lead_both = passed_along(
        jnp.concatenate(
            [
                ssm_input[length - CONV + 1 :],
                state_maps[length - CONV + 1 :].reshape(CONV - 1, map_width),
            ],
            axis=1,
        ),
        "ctx",
        1,
    )
    lead_input = lead_both[:, :inner_width]
    lead_maps = lead_both[:, inner_width:].reshape((CONV - 1,) + state_maps.shape[1:])
    conv_out = causal_conv(ssm_input, lead_input, conv_weight, conv_bias)
    maps_out = causal_conv(state_maps, lead_maps, map_conv, map_bias)
    log_decay = -decay_rate[None, :] * step_size
    running = jnp.cumsum(log_decay.reshape(blocks, BLOCK, head_count), axis=1)
    values = conv_out.reshape(blocks, BLOCK, head_count, HEAD_DIM)
    input_maps = maps_out[:, 0].reshape(blocks, BLOCK, groups, STATE)
    output_maps = maps_out[:, 1].reshape(blocks, BLOCK, groups, STATE)
    block_steps = step_size.reshape(blocks, BLOCK, head_count)
    scores = jnp.einsum(
        "cqgn,csgn->cgqs", output_maps, input_maps, preferred_element_type=jnp.float32
    )
    scores = jnp.broadcast_to(scores[:, :, None], (blocks, groups, repeat, BLOCK, BLOCK)).reshape(
        blocks, head_count, BLOCK, BLOCK
    )
    head_major = jnp.transpose(running, (0, 2, 1))
    gap_log = head_major[:, :, :, None] - head_major[:, :, None, :]
    causal_mask = jnp.tril(jnp.ones((BLOCK, BLOCK), dtype=bool))
    decays = jnp.exp(jnp.where(causal_mask[None, None], gap_log, -1e30))
    step_major = jnp.transpose(block_steps, (0, 2, 1))
    weights = (scores * decays * step_major[:, :, None, :]).astype(jnp.bfloat16)
    within = jnp.einsum("chqs,cshp->cqhp", weights, values, preferred_element_type=jnp.float32)
    to_end = jnp.exp(running[:, -1:, :] - running) * block_steps
    input_heads = jnp.broadcast_to(
        input_maps[:, :, :, None], (blocks, BLOCK, groups, repeat, STATE)
    ).reshape(blocks, BLOCK, head_count, STATE)
    loaded = (input_heads.astype(jnp.float32) * to_end[..., None]).astype(jnp.bfloat16)
    fresh_state = jnp.einsum("cshn,cshp->chnp", loaded, values, preferred_element_type=jnp.float32)
    totals = running[:, -1, :]

    empty_state = jnp.zeros((head_count, STATE, HEAD_DIM), jnp.float32)
    local_enter = []
    carry_state = empty_state
    for block in range(blocks):
        local_enter.append(carry_state)
        carry_state = jnp.exp(totals[block])[:, None, None] * carry_state + fresh_state[block]
    local_end = carry_state
    local_enter = jnp.stack(local_enter)
    device_log = jnp.sum(totals, axis=0)
    before_log, incoming = exclusive_scan(device_log, local_end, "ctx")
    prior_log = jnp.cumsum(totals, axis=0) - totals
    entering = jnp.exp(prior_log)[:, :, None, None] * incoming[None] + local_enter
    carried = entering.astype(jnp.bfloat16).reshape(blocks, groups, repeat, STATE, HEAD_DIM)
    before = jnp.einsum(
        "cqgn,cgrnp->cqgrp", output_maps, carried, preferred_element_type=jnp.float32
    )
    before = jnp.exp(running)[..., None] * before.reshape(blocks, BLOCK, head_count, HEAD_DIM)
    output = within + before + skip_gain[None, None, :, None] * values.astype(jnp.float32)
    flat = with_layout_constraint(output.reshape(length, inner_width), Layout((0, 1)))
    gated = flat * jax.nn.silu(gate_input.astype(jnp.float32))
    grouped = gated.reshape(length, groups, inner_width // groups)
    inverse_rms = lax.rsqrt(jnp.mean(grouped * grouped, axis=2, keepdims=True) + 1e-05)
    normed = lax.optimization_barrier(
        ((grouped * inverse_rms).reshape(length, inner_width) * norm_gain[None, :]).astype(
            jnp.bfloat16
        )
    )
    return scattered_sum(normed, out_weight, "tp")


def solution(mesh):
    in_specs = (
        P("ctx", "tp"),
        P("ctx", "tp"),
        P("ctx", None, "tp"),
        P("ctx", "tp"),
        P("tp"),
        P("tp"),
        P(None, "tp"),
        P("tp"),
        P(None, None, "tp"),
        P(None, "tp"),
        P("tp"),
        P("tp", None),
    )
    out_specs = P(("ctx", "tp"), None)
    return jax.shard_map(local, mesh=mesh, in_specs=in_specs, out_specs=out_specs, check_vma=False)
```

```python
import jax
import jax.numpy as jnp
from jax import lax
from jax.sharding import PartitionSpec as P

HEAD_DIM = 64
STATE = 128
CONV = 4
BLOCK = 128


def passed_along(value, axis, steps):
    count = lax.axis_size(axis)
    first, last = (max(0, -steps), min(count, count - steps))
    return lax.ppermute(value, axis, [(source, source + steps) for source in range(first, last)])


def exclusive_scan(log_total, state, axis):
    count = lax.axis_size(axis)
    heads = state.shape[0]
    rows, cols = state.shape[1:]
    window_log, window_state = log_total, state
    prior_log = jnp.zeros_like(log_total)
    prior_state = jnp.zeros_like(state)
    distance = 1
    while distance < count:
        pairs = [(source, source + distance) for source in range(count - distance)]
        high = window_log.astype(jnp.bfloat16)
        low = (window_log - high.astype(jnp.float32)).astype(jnp.bfloat16)
        log_rows = jnp.pad(jnp.stack([high, low], axis=1), ((0, rows - heads), (0, cols - 2)))
        packed = jnp.concatenate([window_state.astype(jnp.bfloat16), log_rows[None]], axis=0)
        got = lax.ppermute(packed, axis, pairs)
        got_state = got[:heads].astype(jnp.float32)
        got_log = got[heads, :heads, 0].astype(jnp.float32) + got[heads, :heads, 1].astype(jnp.float32)
        prior_state = jnp.exp(prior_log)[:, None, None] * got_state + prior_state
        prior_log = got_log + prior_log
        if 2 * distance < count:
            window_state = jnp.exp(window_log)[:, None, None] * got_state + window_state
            window_log = got_log + window_log
        distance *= 2
    return prior_log, prior_state


def scattered_sum(rows, weight, axis):
    count = lax.axis_size(axis)
    chips = count // 2
    place = lax.axis_index(axis)
    core = place % 2
    chip = place // 2
    length = rows.shape[0]
    share = length // count
    width = weight.shape[1]
    blocks = rows.reshape(chips, 2, share, rows.shape[1])
    sent_rows = lax.dynamic_index_in_dim(blocks, 1 - core, 1, False)
    kept_rows = lax.dynamic_index_in_dim(blocks, core, 1, False)
    sent = jnp.einsum("ysk,kd->ysd", sent_rows, weight, preferred_element_type=jnp.float32)
    swapped = lax.ppermute(
        sent.astype(jnp.bfloat16), axis, [(source, source ^ 1) for source in range(count)]
    )
    first = sorted({(chips - 1) % chips, 1 % chips})
    later = [offset for offset in range(chips) if offset not in first]
    where = {}
    kept = []
    for group in (first, later):
        if not group:
            continue
        picked = jnp.stack(
            [lax.dynamic_index_in_dim(kept_rows, (chip + offset) % chips, 0, False) for offset in group]
        )
        product = jnp.einsum("ysk,kd->ysd", picked, weight, preferred_element_type=jnp.float32)
        kept.append(lax.optimization_barrier(product))
        for index, offset in enumerate(group):
            where[offset] = (len(kept) - 1, index)

    def summed(offset, columns):
        group, index = where[offset % chips]
        own = kept[group][index][:, columns]
        other = lax.dynamic_index_in_dim(swapped, (chip + offset) % chips, 0, False)[:, columns]
        return own + other.astype(jnp.float32)

    half = width // 2
    right_cols, left_cols = slice(0, half), slice(half, width)
    if chips == 1:
        return jnp.concatenate([summed(0, right_cols), summed(0, left_cols)], axis=1).astype(jnp.bfloat16)
    rightward = [(source, (source + 2) % count) for source in range(count)]
    leftward = [(source, (source - 2) % count) for source in range(count)]
    right_acc = summed(-1, right_cols)
    left_acc = summed(1, left_cols)
    for step in range(chips - 1):
        got_right = lax.ppermute(right_acc.astype(jnp.bfloat16), axis, rightward)
        got_left = lax.ppermute(left_acc.astype(jnp.bfloat16), axis, leftward)
        right_acc = summed(-2 - step, right_cols) + got_right.astype(jnp.float32)
        left_acc = summed(2 + step, left_cols) + got_left.astype(jnp.float32)
    return jnp.concatenate([right_acc, left_acc], axis=1).astype(jnp.bfloat16)


def causal_conv(values, lead_rows, weight, bias_term):
    padded = lax.optimization_barrier(
        jnp.concatenate([lead_rows, values], axis=0).astype(jnp.float32)
    )
    length = values.shape[0]
    accum = jnp.zeros(values.shape, jnp.float32) + bias_term
    for offset in range(weight.shape[0]):
        accum = accum + weight[offset] * padded[offset : offset + length]
    return jax.nn.silu(accum).astype(jnp.bfloat16)


def local(
    ssm_input,
    gate_input,
    state_maps,
    step_size,
    decay_rate,
    skip_gain,
    conv_weight,
    conv_bias,
    map_conv,
    map_bias,
    norm_gain,
    out_weight,
):
    length = ssm_input.shape[0]
    head_count = step_size.shape[1]
    inner_width = ssm_input.shape[1]
    groups = state_maps.shape[2] // STATE
    repeat = head_count // groups
    blocks = length // BLOCK
    map_width = state_maps.shape[1] * state_maps.shape[2]
    lead_both = passed_along(
        jnp.concatenate(
            [
                ssm_input[length - CONV + 1 :],
                state_maps[length - CONV + 1 :].reshape(CONV - 1, map_width),
            ],
            axis=1,
        ),
        "ctx",
        1,
    )
    lead_input = lead_both[:, :inner_width]
    lead_maps = lead_both[:, inner_width:].reshape((CONV - 1,) + state_maps.shape[1:])
    conv_out = causal_conv(ssm_input, lead_input, conv_weight, conv_bias)
    maps_out = causal_conv(state_maps, lead_maps, map_conv, map_bias)
    log_decay = -decay_rate[None, :] * step_size
    running = jnp.cumsum(log_decay.reshape(blocks, BLOCK, head_count), axis=1)
    values = conv_out.reshape(blocks, BLOCK, head_count, HEAD_DIM)
    input_maps = maps_out[:, 0].reshape(blocks, BLOCK, groups, STATE)
    output_maps = maps_out[:, 1].reshape(blocks, BLOCK, groups, STATE)
    block_steps = step_size.reshape(blocks, BLOCK, head_count)
    scores = jnp.einsum(
        "cqgn,csgn->cgqs", output_maps, input_maps, preferred_element_type=jnp.float32
    )
    scores = jnp.broadcast_to(scores[:, :, None], (blocks, groups, repeat, BLOCK, BLOCK)).reshape(
        blocks, head_count, BLOCK, BLOCK
    )
    head_major = jnp.transpose(running, (0, 2, 1))
    gap_log = head_major[:, :, :, None] - head_major[:, :, None, :]
    causal_mask = jnp.tril(jnp.ones((BLOCK, BLOCK), dtype=bool))
    decays = jnp.exp(jnp.where(causal_mask[None, None], gap_log, -1e30))
    step_major = jnp.transpose(block_steps, (0, 2, 1))
    weights = (scores * decays * step_major[:, :, None, :]).astype(jnp.bfloat16)
    within = jnp.einsum("chqs,cshp->cqhp", weights, values, preferred_element_type=jnp.float32)
    to_end = jnp.exp(running[:, -1:, :] - running) * block_steps
    input_heads = jnp.broadcast_to(
        input_maps[:, :, :, None], (blocks, BLOCK, groups, repeat, STATE)
    ).reshape(blocks, BLOCK, head_count, STATE)
    loaded = (input_heads.astype(jnp.float32) * to_end[..., None]).astype(jnp.bfloat16)
    fresh_state = jnp.einsum("cshn,cshp->chnp", loaded, values, preferred_element_type=jnp.float32)
    totals = running[:, -1, :]

    empty_state = jnp.zeros((head_count, STATE, HEAD_DIM), jnp.float32)
    local_enter = []
    carry_state = empty_state
    for block in range(blocks):
        local_enter.append(carry_state)
        carry_state = jnp.exp(totals[block])[:, None, None] * carry_state + fresh_state[block]
    local_end = carry_state
    local_enter = jnp.stack(local_enter)
    device_log = jnp.sum(totals, axis=0)
    before_log, incoming = exclusive_scan(device_log, local_end, "ctx")
    prior_log = jnp.cumsum(totals, axis=0) - totals
    entering = jnp.exp(prior_log)[:, :, None, None] * incoming[None] + local_enter
    carried = entering.astype(jnp.bfloat16).reshape(blocks, groups, repeat, STATE, HEAD_DIM)
    before = jnp.einsum(
        "cqgn,cgrnp->cqgrp", output_maps, carried, preferred_element_type=jnp.float32
    )
    before = jnp.exp(running)[..., None] * before.reshape(blocks, BLOCK, head_count, HEAD_DIM)
    output = within + before + skip_gain[None, None, :, None] * values.astype(jnp.float32)
    gated = output.reshape(length, inner_width) * jax.nn.silu(gate_input.astype(jnp.float32))
    grouped = gated.reshape(length, groups, inner_width // groups)
    inverse_rms = lax.rsqrt(jnp.mean(grouped * grouped, axis=2, keepdims=True) + 1e-05)
    normed = lax.optimization_barrier(
        ((grouped * inverse_rms).reshape(length, inner_width) * norm_gain[None, :]).astype(
            jnp.bfloat16
        )
    )
    return scattered_sum(normed, out_weight, "tp")


def solution(mesh):
    in_specs = (
        P("ctx", "tp"),
        P("ctx", "tp"),
        P("ctx", None, "tp"),
        P("ctx", "tp"),
        P("tp"),
        P("tp"),
        P(None, "tp"),
        P("tp"),
        P(None, None, "tp"),
        P(None, "tp"),
        P("tp"),
        P("tp", None),
    )
    out_specs = P(("ctx", "tp"), None)
    return jax.shard_map(local, mesh=mesh, in_specs=in_specs, out_specs=out_specs, check_vma=False)
```

```python
import jax
import jax.numpy as jnp
from jax import lax
from jax.sharding import PartitionSpec as P

HEAD_DIM = 64
STATE = 128
CONV = 4
BLOCK = 128


def passed_along(value, axis, steps):
    count = lax.axis_size(axis)
    first, last = (max(0, -steps), min(count, count - steps))
    return lax.ppermute(value, axis, [(source, source + steps) for source in range(first, last)])


def exclusive_scan(log_total, state, axis):
    count = lax.axis_size(axis)
    heads = state.shape[0]
    rows, cols = state.shape[1:]
    window_log, window_state = log_total, state
    prior_log = jnp.zeros_like(log_total)
    prior_state = jnp.zeros_like(state)
    distance = 1
    while distance < count:
        pairs = [(source, source + distance) for source in range(count - distance)]
        high = window_log.astype(jnp.bfloat16)
        low = (window_log - high.astype(jnp.float32)).astype(jnp.bfloat16)
        log_rows = jnp.pad(jnp.stack([high, low], axis=1), ((0, rows - heads), (0, cols - 2)))
        packed = jnp.concatenate([window_state.astype(jnp.bfloat16), log_rows[None]], axis=0)
        got = lax.ppermute(packed, axis, pairs)
        got_state = got[:heads].astype(jnp.float32)
        got_log = got[heads, :heads, 0].astype(jnp.float32) + got[heads, :heads, 1].astype(jnp.float32)
        prior_state = jnp.exp(prior_log)[:, None, None] * got_state + prior_state
        prior_log = got_log + prior_log
        if 2 * distance < count:
            window_state = jnp.exp(window_log)[:, None, None] * got_state + window_state
            window_log = got_log + window_log
        distance *= 2
    return prior_log, prior_state


def scattered_sum(rows, weight, axis):
    count = lax.axis_size(axis)
    chips = count // 2
    place = lax.axis_index(axis)
    core = place % 2
    chip = place // 2
    length = rows.shape[0]
    share = length // count
    width = weight.shape[1]
    blocks = rows.reshape(chips, 2, share, rows.shape[1])
    product = jnp.einsum("ycsk,kd->ycsd", blocks, weight, preferred_element_type=jnp.float32)
    sent = lax.dynamic_index_in_dim(product, 1 - core, 1, False)
    swapped = lax.ppermute(
        sent.astype(jnp.bfloat16), axis, [(source, source ^ 1) for source in range(count)]
    )
    kept = lax.dynamic_index_in_dim(product, core, 1, False)
    summed = kept + swapped.astype(jnp.float32)
    if chips == 1:
        return summed[0].astype(jnp.bfloat16)
    half = width // 2
    rightward = [(source, (source + 2) % count) for source in range(count)]
    leftward = [(source, (source - 2) % count) for source in range(count)]
    right_acc = lax.dynamic_index_in_dim(summed, (chip - 1) % chips, 0, False)[:, :half]
    left_acc = lax.dynamic_index_in_dim(summed, (chip + 1) % chips, 0, False)[:, half:]
    for step in range(chips - 1):
        got_right = lax.ppermute(right_acc.astype(jnp.bfloat16), axis, rightward)
        got_left = lax.ppermute(left_acc.astype(jnp.bfloat16), axis, leftward)
        right_own = lax.dynamic_index_in_dim(summed, (chip - 2 - step) % chips, 0, False)[:, :half]
        left_own = lax.dynamic_index_in_dim(summed, (chip + 2 + step) % chips, 0, False)[:, half:]
        right_acc = right_own + got_right.astype(jnp.float32)
        left_acc = left_own + got_left.astype(jnp.float32)
    return jnp.concatenate([right_acc, left_acc], axis=1).astype(jnp.bfloat16)


def causal_conv(values, lead_rows, weight, bias_term):
    padded = lax.optimization_barrier(
        jnp.concatenate([lead_rows, values], axis=0).astype(jnp.float32)
    )
    length = values.shape[0]
    accum = jnp.zeros(values.shape, jnp.float32) + bias_term
    for offset in range(weight.shape[0]):
        accum = accum + weight[offset] * padded[offset : offset + length]
    return jax.nn.silu(accum).astype(jnp.bfloat16)


def local(
    ssm_input,
    gate_input,
    state_maps,
    step_size,
    decay_rate,
    skip_gain,
    conv_weight,
    conv_bias,
    map_conv,
    map_bias,
    norm_gain,
    out_weight,
):
    length = ssm_input.shape[0]
    head_count = step_size.shape[1]
    inner_width = ssm_input.shape[1]
    groups = state_maps.shape[2] // STATE
    repeat = head_count // groups
    blocks = length // BLOCK
    map_width = state_maps.shape[1] * state_maps.shape[2]
    lead_both = passed_along(
        jnp.concatenate(
            [
                ssm_input[length - CONV + 1 :],
                state_maps[length - CONV + 1 :].reshape(CONV - 1, map_width),
            ],
            axis=1,
        ),
        "ctx",
        1,
    )
    lead_input = lead_both[:, :inner_width]
    lead_maps = lead_both[:, inner_width:].reshape((CONV - 1,) + state_maps.shape[1:])
    conv_out = causal_conv(ssm_input, lead_input, conv_weight, conv_bias)
    maps_out = causal_conv(state_maps, lead_maps, map_conv, map_bias)
    log_decay = -decay_rate[None, :] * step_size
    running = jnp.cumsum(log_decay.reshape(blocks, BLOCK, head_count), axis=1)
    values = conv_out.reshape(blocks, BLOCK, head_count, HEAD_DIM)
    input_maps = maps_out[:, 0].reshape(blocks, BLOCK, groups, STATE)
    output_maps = maps_out[:, 1].reshape(blocks, BLOCK, groups, STATE)
    block_steps = step_size.reshape(blocks, BLOCK, head_count)
    scores = jnp.einsum(
        "cqgn,csgn->cgqs", output_maps, input_maps, preferred_element_type=jnp.float32
    )
    scores = jnp.broadcast_to(scores[:, :, None], (blocks, groups, repeat, BLOCK, BLOCK)).reshape(
        blocks, head_count, BLOCK, BLOCK
    )
    head_major = jnp.transpose(running, (0, 2, 1))
    gap_log = head_major[:, :, :, None] - head_major[:, :, None, :]
    causal_mask = jnp.tril(jnp.ones((BLOCK, BLOCK), dtype=bool))
    decays = jnp.exp(jnp.where(causal_mask[None, None], gap_log, -1e30))
    step_major = jnp.transpose(block_steps, (0, 2, 1))
    weights = (scores * decays * step_major[:, :, None, :]).astype(jnp.bfloat16)
    within = jnp.einsum("chqs,cshp->cqhp", weights, values, preferred_element_type=jnp.float32)
    to_end = jnp.exp(running[:, -1:, :] - running) * block_steps
    input_heads = jnp.broadcast_to(
        input_maps[:, :, :, None], (blocks, BLOCK, groups, repeat, STATE)
    ).reshape(blocks, BLOCK, head_count, STATE)
    loaded = (input_heads.astype(jnp.float32) * to_end[..., None]).astype(jnp.bfloat16)
    fresh_state = jnp.einsum("cshn,cshp->chnp", loaded, values, preferred_element_type=jnp.float32)
    totals = running[:, -1, :]

    empty_state = jnp.zeros((head_count, STATE, HEAD_DIM), jnp.float32)
    local_enter = []
    carry_state = empty_state
    for block in range(blocks):
        local_enter.append(carry_state)
        carry_state = jnp.exp(totals[block])[:, None, None] * carry_state + fresh_state[block]
    local_end = carry_state
    local_enter = jnp.stack(local_enter)
    device_log = jnp.sum(totals, axis=0)
    before_log, incoming = exclusive_scan(device_log, local_end, "ctx")
    prior_log = jnp.cumsum(totals, axis=0) - totals
    entering = jnp.exp(prior_log)[:, :, None, None] * incoming[None] + local_enter
    carried = entering.astype(jnp.bfloat16).reshape(blocks, groups, repeat, STATE, HEAD_DIM)
    before = jnp.einsum(
        "cqgn,cgrnp->cqgrp", output_maps, carried, preferred_element_type=jnp.float32
    )
    before = jnp.exp(running)[..., None] * before.reshape(blocks, BLOCK, head_count, HEAD_DIM)
    output = within + before + skip_gain[None, None, :, None] * values.astype(jnp.float32)
    gated = output.reshape(length, inner_width) * jax.nn.silu(gate_input.astype(jnp.float32))
    grouped = gated.reshape(length, groups, inner_width // groups)
    inverse_rms = lax.rsqrt(jnp.mean(grouped * grouped, axis=2, keepdims=True) + 1e-05)
    normed = lax.optimization_barrier(
        ((grouped * inverse_rms).reshape(length, inner_width) * norm_gain[None, :]).astype(
            jnp.bfloat16
        )
    )
    return scattered_sum(normed, out_weight, "tp")


def solution(mesh):
    in_specs = (
        P("ctx", "tp"),
        P("ctx", "tp"),
        P("ctx", None, "tp"),
        P("ctx", "tp"),
        P("tp"),
        P("tp"),
        P(None, "tp"),
        P("tp"),
        P(None, None, "tp"),
        P(None, "tp"),
        P("tp"),
        P("tp", None),
    )
    out_specs = P(("ctx", "tp"), None)
    return jax.shard_map(local, mesh=mesh, in_specs=in_specs, out_specs=out_specs, check_vma=False)
```

```python
import jax
import jax.numpy as jnp
from jax import lax
from jax.sharding import PartitionSpec as P

HEAD_DIM = 64
STATE = 128
CONV = 4
BLOCK = 128


def passed_along(value, axis, steps):
    count = lax.axis_size(axis)
    first, last = (max(0, -steps), min(count, count - steps))
    return lax.ppermute(value, axis, [(source, source + steps) for source in range(first, last)])


def exclusive_scan(log_total, state, axis):
    count = lax.axis_size(axis)
    heads = state.shape[0]
    rows, cols = state.shape[1:]
    window_log, window_state = log_total, state
    prior_log = jnp.zeros_like(log_total)
    prior_state = jnp.zeros_like(state)
    distance = 1
    while distance < count:
        pairs = [(source, source + distance) for source in range(count - distance)]
        high = window_log.astype(jnp.bfloat16)
        low = (window_log - high.astype(jnp.float32)).astype(jnp.bfloat16)
        log_rows = jnp.pad(jnp.stack([high, low], axis=1), ((0, rows - heads), (0, cols - 2)))
        packed = jnp.concatenate([window_state.astype(jnp.bfloat16), log_rows[None]], axis=0)
        got = lax.ppermute(packed, axis, pairs)
        got_state = got[:heads].astype(jnp.float32)
        got_log = got[heads, :heads, 0].astype(jnp.float32) + got[heads, :heads, 1].astype(jnp.float32)
        prior_state = jnp.exp(prior_log)[:, None, None] * got_state + prior_state
        prior_log = got_log + prior_log
        if 2 * distance < count:
            window_state = jnp.exp(window_log)[:, None, None] * got_state + window_state
            window_log = got_log + window_log
        distance *= 2
    return prior_log, prior_state


def scattered_sum(rows, weight, axis):
    count = lax.axis_size(axis)
    chips = count // 2
    place = lax.axis_index(axis)
    core = place % 2
    chip = place // 2
    length = rows.shape[0]
    share = length // count
    half = weight.shape[1] // 2
    blocks = rows.reshape(chips, 2, share, rows.shape[1])
    swap = [(source, source ^ 1) for source in range(count)]

    def summed_half(columns):
        product = jnp.einsum(
            "ycsk,kd->ycsd", blocks, weight[:, columns], preferred_element_type=jnp.float32
        )
        sent = lax.dynamic_index_in_dim(product, 1 - core, 1, False)
        swapped = lax.ppermute(sent.astype(jnp.bfloat16), axis, swap)
        kept = lax.dynamic_index_in_dim(product, core, 1, False)
        return kept + swapped.astype(jnp.float32)

    summed_right = summed_half(slice(0, half))
    summed_left = summed_half(slice(half, 2 * half))
    if chips == 1:
        return jnp.concatenate([summed_right[0], summed_left[0]], axis=1).astype(jnp.bfloat16)
    rightward = [(source, (source + 2) % count) for source in range(count)]
    leftward = [(source, (source - 2) % count) for source in range(count)]
    right_acc = lax.dynamic_index_in_dim(summed_right, (chip - 1) % chips, 0, False)
    left_acc = lax.dynamic_index_in_dim(summed_left, (chip + 1) % chips, 0, False)
    for step in range(chips - 1):
        got_right = lax.ppermute(right_acc.astype(jnp.bfloat16), axis, rightward)
        got_left = lax.ppermute(left_acc.astype(jnp.bfloat16), axis, leftward)
        right_own = lax.dynamic_index_in_dim(summed_right, (chip - 2 - step) % chips, 0, False)
        left_own = lax.dynamic_index_in_dim(summed_left, (chip + 2 + step) % chips, 0, False)
        right_acc = right_own + got_right.astype(jnp.float32)
        left_acc = left_own + got_left.astype(jnp.float32)
    return jnp.concatenate([right_acc, left_acc], axis=1).astype(jnp.bfloat16)


def causal_conv(values, lead_rows, weight, bias_term):
    padded = lax.optimization_barrier(
        jnp.concatenate([lead_rows, values], axis=0).astype(jnp.float32)
    )
    length = values.shape[0]
    accum = jnp.zeros(values.shape, jnp.float32) + bias_term
    for offset in range(weight.shape[0]):
        accum = accum + weight[offset] * padded[offset : offset + length]
    return jax.nn.silu(accum).astype(jnp.bfloat16)


def local(
    ssm_input,
    gate_input,
    state_maps,
    step_size,
    decay_rate,
    skip_gain,
    conv_weight,
    conv_bias,
    map_conv,
    map_bias,
    norm_gain,
    out_weight,
):
    length = ssm_input.shape[0]
    head_count = step_size.shape[1]
    inner_width = ssm_input.shape[1]
    groups = state_maps.shape[2] // STATE
    repeat = head_count // groups
    blocks = length // BLOCK
    map_width = state_maps.shape[1] * state_maps.shape[2]
    lead_both = passed_along(
        jnp.concatenate(
            [
                ssm_input[length - CONV + 1 :],
                state_maps[length - CONV + 1 :].reshape(CONV - 1, map_width),
            ],
            axis=1,
        ),
        "ctx",
        1,
    )
    lead_input = lead_both[:, :inner_width]
    lead_maps = lead_both[:, inner_width:].reshape((CONV - 1,) + state_maps.shape[1:])
    conv_out = causal_conv(ssm_input, lead_input, conv_weight, conv_bias)
    maps_out = causal_conv(state_maps, lead_maps, map_conv, map_bias)
    log_decay = -decay_rate[None, :] * step_size
    running = jnp.cumsum(log_decay.reshape(blocks, BLOCK, head_count), axis=1)
    values = conv_out.reshape(blocks, BLOCK, head_count, HEAD_DIM)
    input_maps = maps_out[:, 0].reshape(blocks, BLOCK, groups, STATE)
    output_maps = maps_out[:, 1].reshape(blocks, BLOCK, groups, STATE)
    block_steps = step_size.reshape(blocks, BLOCK, head_count)
    scores = jnp.einsum(
        "cqgn,csgn->cgqs", output_maps, input_maps, preferred_element_type=jnp.float32
    )
    scores = jnp.broadcast_to(scores[:, :, None], (blocks, groups, repeat, BLOCK, BLOCK)).reshape(
        blocks, head_count, BLOCK, BLOCK
    )
    head_major = jnp.transpose(running, (0, 2, 1))
    gap_log = head_major[:, :, :, None] - head_major[:, :, None, :]
    causal_mask = jnp.tril(jnp.ones((BLOCK, BLOCK), dtype=bool))
    decays = jnp.exp(jnp.where(causal_mask[None, None], gap_log, -1e30))
    step_major = jnp.transpose(block_steps, (0, 2, 1))
    weights = (scores * decays * step_major[:, :, None, :]).astype(jnp.bfloat16)
    within = jnp.einsum("chqs,cshp->cqhp", weights, values, preferred_element_type=jnp.float32)
    to_end = jnp.exp(running[:, -1:, :] - running) * block_steps
    input_heads = jnp.broadcast_to(
        input_maps[:, :, :, None], (blocks, BLOCK, groups, repeat, STATE)
    ).reshape(blocks, BLOCK, head_count, STATE)
    loaded = (input_heads.astype(jnp.float32) * to_end[..., None]).astype(jnp.bfloat16)
    fresh_state = jnp.einsum("cshn,cshp->chnp", loaded, values, preferred_element_type=jnp.float32)
    totals = running[:, -1, :]

    empty_state = jnp.zeros((head_count, STATE, HEAD_DIM), jnp.float32)
    local_enter = []
    carry_state = empty_state
    for block in range(blocks):
        local_enter.append(carry_state)
        carry_state = jnp.exp(totals[block])[:, None, None] * carry_state + fresh_state[block]
    local_end = carry_state
    local_enter = jnp.stack(local_enter)
    device_log = jnp.sum(totals, axis=0)
    before_log, incoming = exclusive_scan(device_log, local_end, "ctx")
    prior_log = jnp.cumsum(totals, axis=0) - totals
    entering = jnp.exp(prior_log)[:, :, None, None] * incoming[None] + local_enter
    carried = entering.astype(jnp.bfloat16).reshape(blocks, groups, repeat, STATE, HEAD_DIM)
    before = jnp.einsum(
        "cqgn,cgrnp->cqgrp", output_maps, carried, preferred_element_type=jnp.float32
    )
    before = jnp.exp(running)[..., None] * before.reshape(blocks, BLOCK, head_count, HEAD_DIM)
    output = within + before + skip_gain[None, None, :, None] * values.astype(jnp.float32)
    gated = output.reshape(length, inner_width) * jax.nn.silu(gate_input.astype(jnp.float32))
    grouped = gated.reshape(length, groups, inner_width // groups)
    inverse_rms = lax.rsqrt(jnp.mean(grouped * grouped, axis=2, keepdims=True) + 1e-05)
    normed = lax.optimization_barrier(
        ((grouped * inverse_rms).reshape(length, inner_width) * norm_gain[None, :]).astype(
            jnp.bfloat16
        )
    )
    return scattered_sum(normed, out_weight, "tp")


def solution(mesh):
    in_specs = (
        P("ctx", "tp"),
        P("ctx", "tp"),
        P("ctx", None, "tp"),
        P("ctx", "tp"),
        P("tp"),
        P("tp"),
        P(None, "tp"),
        P("tp"),
        P(None, None, "tp"),
        P(None, "tp"),
        P("tp"),
        P("tp", None),
    )
    out_specs = P(("ctx", "tp"), None)
    return jax.shard_map(local, mesh=mesh, in_specs=in_specs, out_specs=out_specs, check_vma=False)
```

```python
import jax
import jax.numpy as jnp
from jax import lax
from jax.sharding import PartitionSpec as P

HEAD_DIM = 64
STATE = 128
CONV = 4
BLOCK = 128


def passed_along(value, axis, steps):
    count = lax.axis_size(axis)
    first, last = (max(0, -steps), min(count, count - steps))
    return lax.ppermute(value, axis, [(source, source + steps) for source in range(first, last)])


def exclusive_scan(log_total, state, axis):
    count = lax.axis_size(axis)
    heads = state.shape[0]
    rows, cols = state.shape[1:]
    window_log, window_state = log_total, state
    prior_log = jnp.zeros_like(log_total)
    prior_state = jnp.zeros_like(state)
    distance = 1
    while distance < count:
        pairs = [(source, source + distance) for source in range(count - distance)]
        high = window_log.astype(jnp.bfloat16)
        low = (window_log - high.astype(jnp.float32)).astype(jnp.bfloat16)
        log_rows = jnp.pad(jnp.stack([high, low], axis=1), ((0, rows - heads), (0, cols - 2)))
        packed = jnp.concatenate([window_state.astype(jnp.bfloat16), log_rows[None]], axis=0)
        got = lax.ppermute(packed, axis, pairs)
        got_state = got[:heads].astype(jnp.float32)
        got_log = got[heads, :heads, 0].astype(jnp.float32) + got[heads, :heads, 1].astype(jnp.float32)
        prior_state = jnp.exp(prior_log)[:, None, None] * got_state + prior_state
        prior_log = got_log + prior_log
        if 2 * distance < count:
            window_state = jnp.exp(window_log)[:, None, None] * got_state + window_state
            window_log = got_log + window_log
        distance *= 2
    return prior_log, prior_state


def scattered_sum(rows, weight, axis):
    count = lax.axis_size(axis)
    chips = count // 2
    place = lax.axis_index(axis)
    core = place % 2
    chip = place // 2
    length = rows.shape[0]
    share = length // count
    half = weight.shape[1] // 2
    blocks = rows.reshape(chips, 2, share, rows.shape[1])
    swap = [(source, source ^ 1) for source in range(count)]

    def summed_half(columns):
        product = jnp.einsum(
            "ycsk,kd->ycsd", blocks, weight[:, columns], preferred_element_type=jnp.float32
        )
        sent = lax.dynamic_index_in_dim(product, 1 - core, 1, False)
        swapped = lax.ppermute(sent.astype(jnp.bfloat16), axis, swap)
        kept = lax.dynamic_index_in_dim(product, core, 1, False)
        return kept + swapped.astype(jnp.float32)

    summed_right = summed_half(slice(0, half))
    summed_left = summed_half(slice(half, 2 * half))
    if chips == 1:
        return jnp.concatenate([summed_right[0], summed_left[0]], axis=1).astype(jnp.bfloat16)
    rightward = [(source, (source + 2) % count) for source in range(count)]
    leftward = [(source, (source - 2) % count) for source in range(count)]
    right_acc = lax.dynamic_index_in_dim(summed_right, (chip - 1) % chips, 0, False)
    left_acc = lax.dynamic_index_in_dim(summed_left, (chip + 1) % chips, 0, False)
    for step in range(chips - 1):
        got_right = lax.ppermute(right_acc.astype(jnp.bfloat16), axis, rightward)
        got_left = lax.ppermute(left_acc.astype(jnp.bfloat16), axis, leftward)
        right_own = lax.dynamic_index_in_dim(summed_right, (chip - 2 - step) % chips, 0, False)
        left_own = lax.dynamic_index_in_dim(summed_left, (chip + 2 + step) % chips, 0, False)
        right_acc = right_own + got_right.astype(jnp.float32)
        left_acc = left_own + got_left.astype(jnp.float32)
    return jnp.concatenate([right_acc, left_acc], axis=1).astype(jnp.bfloat16)


def causal_conv(values, lead_rows, weight, bias_term):
    padded = lax.optimization_barrier(
        jnp.concatenate([lead_rows, values], axis=0).astype(jnp.float32)
    )
    length = values.shape[0]
    accum = jnp.zeros(values.shape, jnp.float32) + bias_term
    for offset in range(weight.shape[0]):
        accum = accum + weight[offset] * padded[offset : offset + length]
    return jax.nn.silu(accum).astype(jnp.bfloat16)


def local(
    ssm_input,
    gate_input,
    state_maps,
    step_size,
    decay_rate,
    skip_gain,
    conv_weight,
    conv_bias,
    map_conv,
    map_bias,
    norm_gain,
    out_weight,
):
    length = ssm_input.shape[0]
    head_count = step_size.shape[1]
    inner_width = ssm_input.shape[1]
    groups = state_maps.shape[2] // STATE
    repeat = head_count // groups
    blocks = length // BLOCK
    map_width = state_maps.shape[1] * state_maps.shape[2]
    lead_both = passed_along(
        jnp.concatenate(
            [
                ssm_input[length - CONV + 1 :],
                state_maps[length - CONV + 1 :].reshape(CONV - 1, map_width),
            ],
            axis=1,
        ),
        "ctx",
        1,
    )
    lead_input = lead_both[:, :inner_width]
    lead_maps = lead_both[:, inner_width:].reshape((CONV - 1,) + state_maps.shape[1:])
    conv_out = causal_conv(ssm_input, lead_input, conv_weight, conv_bias)
    maps_out = causal_conv(state_maps, lead_maps, map_conv, map_bias)
    log_decay = -decay_rate[None, :] * step_size
    running = jnp.cumsum(log_decay.reshape(blocks, BLOCK, head_count), axis=1)
    values = conv_out.reshape(blocks, BLOCK, head_count, HEAD_DIM)
    input_maps = maps_out[:, 0].reshape(blocks, BLOCK, groups, STATE)
    output_maps = maps_out[:, 1].reshape(blocks, BLOCK, groups, STATE)
    block_steps = step_size.reshape(blocks, BLOCK, head_count)
    scores = jnp.einsum(
        "cqgn,csgn->cgqs", output_maps, input_maps, preferred_element_type=jnp.float32
    )
    scores = jnp.broadcast_to(scores[:, :, None], (blocks, groups, repeat, BLOCK, BLOCK)).reshape(
        blocks, head_count, BLOCK, BLOCK
    )
    head_major = jnp.transpose(running, (0, 2, 1))
    gap_log = head_major[:, :, :, None] - head_major[:, :, None, :]
    causal_mask = jnp.tril(jnp.ones((BLOCK, BLOCK), dtype=bool))
    decays = jnp.exp(jnp.where(causal_mask[None, None], gap_log, -1e30))
    step_major = jnp.transpose(block_steps, (0, 2, 1))
    weights = (scores * decays * step_major[:, :, None, :]).astype(jnp.bfloat16)
    within = jnp.einsum("chqs,cshp->cqhp", weights, values, preferred_element_type=jnp.float32)
    to_end = jnp.exp(running[:, -1:, :] - running) * block_steps
    input_heads = jnp.broadcast_to(
        input_maps[:, :, :, None], (blocks, BLOCK, groups, repeat, STATE)
    ).reshape(blocks, BLOCK, head_count, STATE)
    loaded = (input_heads.astype(jnp.float32) * to_end[..., None]).astype(jnp.bfloat16)
    fresh_state = jnp.einsum("cshn,cshp->chnp", loaded, values, preferred_element_type=jnp.float32)
    totals = running[:, -1, :]

    empty_state = jnp.zeros((head_count, STATE, HEAD_DIM), jnp.float32)
    local_enter = []
    carry_state = empty_state
    for block in range(blocks):
        local_enter.append(carry_state)
        carry_state = jnp.exp(totals[block])[:, None, None] * carry_state + fresh_state[block]
    local_end = carry_state
    local_enter = jnp.stack(local_enter)
    device_log = jnp.sum(totals, axis=0)
    before_log, incoming = exclusive_scan(device_log, local_end, "ctx")
    prior_log = jnp.cumsum(totals, axis=0) - totals
    entering = jnp.exp(prior_log)[:, :, None, None] * incoming[None] + local_enter
    carried = entering.astype(jnp.bfloat16).reshape(blocks, groups, repeat, STATE, HEAD_DIM)
    before = jnp.einsum(
        "cqgn,cgrnp->cqgrp", output_maps, carried, preferred_element_type=jnp.float32
    )
    before = jnp.exp(running)[..., None] * before.reshape(blocks, BLOCK, head_count, HEAD_DIM)
    output = within + before + skip_gain[None, None, :, None] * values.astype(jnp.float32)
    stored = lax.optimization_barrier(output.reshape(length, inner_width).astype(jnp.bfloat16))
    gated = stored.astype(jnp.float32) * jax.nn.silu(gate_input.astype(jnp.float32))
    grouped = gated.reshape(length, groups, inner_width // groups)
    inverse_rms = lax.rsqrt(jnp.mean(grouped * grouped, axis=2, keepdims=True) + 1e-05)
    normed = lax.optimization_barrier(
        ((grouped * inverse_rms).reshape(length, inner_width) * norm_gain[None, :]).astype(
            jnp.bfloat16
        )
    )
    return scattered_sum(normed, out_weight, "tp")


def solution(mesh):
    in_specs = (
        P("ctx", "tp"),
        P("ctx", "tp"),
        P("ctx", None, "tp"),
        P("ctx", "tp"),
        P("tp"),
        P("tp"),
        P(None, "tp"),
        P("tp"),
        P(None, None, "tp"),
        P(None, "tp"),
        P("tp"),
        P("tp", None),
    )
    out_specs = P(("ctx", "tp"), None)
    return jax.shard_map(local, mesh=mesh, in_specs=in_specs, out_specs=out_specs, check_vma=False)
```

```python
import jax
import jax.numpy as jnp
from jax import lax
from jax.sharding import PartitionSpec as P

HEAD_DIM = 64
STATE = 128
CONV = 4
BLOCK = 128


def passed_along(value, axis, steps):
    count = lax.axis_size(axis)
    first, last = (max(0, -steps), min(count, count - steps))
    return lax.ppermute(value, axis, [(source, source + steps) for source in range(first, last)])


def exclusive_scan(log_total, state, axis):
    count = lax.axis_size(axis)
    heads = state.shape[0]
    rows, cols = state.shape[1:]
    window_log, window_state = log_total, state
    prior_log = jnp.zeros_like(log_total)
    prior_state = jnp.zeros_like(state)
    distance = 1
    while distance < count:
        pairs = [(source, source + distance) for source in range(count - distance)]
        high = window_log.astype(jnp.bfloat16)
        low = (window_log - high.astype(jnp.float32)).astype(jnp.bfloat16)
        log_rows = jnp.pad(jnp.stack([high, low], axis=1), ((0, rows - heads), (0, cols - 2)))
        packed = jnp.concatenate([window_state.astype(jnp.bfloat16), log_rows[None]], axis=0)
        got = lax.ppermute(packed, axis, pairs)
        got_state = got[:heads].astype(jnp.float32)
        got_log = got[heads, :heads, 0].astype(jnp.float32) + got[heads, :heads, 1].astype(jnp.float32)
        prior_state = jnp.exp(prior_log)[:, None, None] * got_state + prior_state
        prior_log = got_log + prior_log
        if 2 * distance < count:
            window_state = jnp.exp(window_log)[:, None, None] * got_state + window_state
            window_log = got_log + window_log
        distance *= 2
    return prior_log, prior_state


def scattered_sum(rows, weight, axis):
    count = lax.axis_size(axis)
    chips = count // 2
    place = lax.axis_index(axis)
    core = place % 2
    chip = place // 2
    length = rows.shape[0]
    share = length // count
    half = weight.shape[1] // 2
    blocks = rows.reshape(chips, 2, share, rows.shape[1])
    sent_rows = lax.dynamic_index_in_dim(blocks, 1 - core, 1, False)
    kept_rows = lax.dynamic_index_in_dim(blocks, core, 1, False)
    swap = [(source, source ^ 1) for source in range(count)]

    def summed_half(columns):
        part = weight[:, columns]
        sent = jnp.einsum("ysk,kd->ysd", sent_rows, part, preferred_element_type=jnp.float32)
        swapped = lax.ppermute(sent.astype(jnp.bfloat16), axis, swap)
        kept = lax.optimization_barrier(
            jnp.einsum("ysk,kd->ysd", kept_rows, part, preferred_element_type=jnp.float32)
        )
        return kept + swapped.astype(jnp.float32)

    summed_right = summed_half(slice(0, half))
    summed_left = summed_half(slice(half, 2 * half))
    if chips == 1:
        return jnp.concatenate([summed_right[0], summed_left[0]], axis=1).astype(jnp.bfloat16)
    rightward = [(source, (source + 2) % count) for source in range(count)]
    leftward = [(source, (source - 2) % count) for source in range(count)]
    right_acc = lax.dynamic_index_in_dim(summed_right, (chip - 1) % chips, 0, False)
    left_acc = lax.dynamic_index_in_dim(summed_left, (chip + 1) % chips, 0, False)
    for step in range(chips - 1):
        got_right = lax.ppermute(right_acc.astype(jnp.bfloat16), axis, rightward)
        got_left = lax.ppermute(left_acc.astype(jnp.bfloat16), axis, leftward)
        right_own = lax.dynamic_index_in_dim(summed_right, (chip - 2 - step) % chips, 0, False)
        left_own = lax.dynamic_index_in_dim(summed_left, (chip + 2 + step) % chips, 0, False)
        right_acc = right_own + got_right.astype(jnp.float32)
        left_acc = left_own + got_left.astype(jnp.float32)
    return jnp.concatenate([right_acc, left_acc], axis=1).astype(jnp.bfloat16)


def causal_conv(values, lead_rows, weight, bias_term):
    padded = lax.optimization_barrier(
        jnp.concatenate([lead_rows, values], axis=0).astype(jnp.float32)
    )
    length = values.shape[0]
    accum = jnp.zeros(values.shape, jnp.float32) + bias_term
    for offset in range(weight.shape[0]):
        accum = accum + weight[offset] * padded[offset : offset + length]
    return jax.nn.silu(accum).astype(jnp.bfloat16)


def local(
    ssm_input,
    gate_input,
    state_maps,
    step_size,
    decay_rate,
    skip_gain,
    conv_weight,
    conv_bias,
    map_conv,
    map_bias,
    norm_gain,
    out_weight,
):
    length = ssm_input.shape[0]
    head_count = step_size.shape[1]
    inner_width = ssm_input.shape[1]
    groups = state_maps.shape[2] // STATE
    repeat = head_count // groups
    blocks = length // BLOCK
    map_width = state_maps.shape[1] * state_maps.shape[2]
    lead_both = passed_along(
        jnp.concatenate(
            [
                ssm_input[length - CONV + 1 :],
                state_maps[length - CONV + 1 :].reshape(CONV - 1, map_width),
            ],
            axis=1,
        ),
        "ctx",
        1,
    )
    lead_input = lead_both[:, :inner_width]
    lead_maps = lead_both[:, inner_width:].reshape((CONV - 1,) + state_maps.shape[1:])
    conv_out = causal_conv(ssm_input, lead_input, conv_weight, conv_bias)
    maps_out = causal_conv(state_maps, lead_maps, map_conv, map_bias)
    log_decay = -decay_rate[None, :] * step_size
    running = jnp.cumsum(log_decay.reshape(blocks, BLOCK, head_count), axis=1)
    values = conv_out.reshape(blocks, BLOCK, head_count, HEAD_DIM)
    input_maps = maps_out[:, 0].reshape(blocks, BLOCK, groups, STATE)
    output_maps = maps_out[:, 1].reshape(blocks, BLOCK, groups, STATE)
    block_steps = step_size.reshape(blocks, BLOCK, head_count)
    scores = jnp.einsum(
        "cqgn,csgn->cgqs", output_maps, input_maps, preferred_element_type=jnp.float32
    )
    scores = jnp.broadcast_to(scores[:, :, None], (blocks, groups, repeat, BLOCK, BLOCK)).reshape(
        blocks, head_count, BLOCK, BLOCK
    )
    head_major = jnp.transpose(running, (0, 2, 1))
    gap_log = head_major[:, :, :, None] - head_major[:, :, None, :]
    causal_mask = jnp.tril(jnp.ones((BLOCK, BLOCK), dtype=bool))
    decays = jnp.exp(jnp.where(causal_mask[None, None], gap_log, -1e30))
    step_major = jnp.transpose(block_steps, (0, 2, 1))
    weights = (scores * decays * step_major[:, :, None, :]).astype(jnp.bfloat16)
    within = jnp.einsum("chqs,cshp->cqhp", weights, values, preferred_element_type=jnp.float32)
    to_end = jnp.exp(running[:, -1:, :] - running) * block_steps
    input_heads = jnp.broadcast_to(
        input_maps[:, :, :, None], (blocks, BLOCK, groups, repeat, STATE)
    ).reshape(blocks, BLOCK, head_count, STATE)
    loaded = (input_heads.astype(jnp.float32) * to_end[..., None]).astype(jnp.bfloat16)
    fresh_state = jnp.einsum("cshn,cshp->chnp", loaded, values, preferred_element_type=jnp.float32)
    totals = running[:, -1, :]

    empty_state = jnp.zeros((head_count, STATE, HEAD_DIM), jnp.float32)
    local_enter = []
    carry_state = empty_state
    for block in range(blocks):
        local_enter.append(carry_state)
        carry_state = jnp.exp(totals[block])[:, None, None] * carry_state + fresh_state[block]
    local_end = carry_state
    local_enter = jnp.stack(local_enter)
    device_log = jnp.sum(totals, axis=0)
    before_log, incoming = exclusive_scan(device_log, local_end, "ctx")
    prior_log = jnp.cumsum(totals, axis=0) - totals
    entering = jnp.exp(prior_log)[:, :, None, None] * incoming[None] + local_enter
    carried = entering.astype(jnp.bfloat16).reshape(blocks, groups, repeat, STATE, HEAD_DIM)
    before = jnp.einsum(
        "cqgn,cgrnp->cqgrp", output_maps, carried, preferred_element_type=jnp.float32
    )
    before = jnp.exp(running)[..., None] * before.reshape(blocks, BLOCK, head_count, HEAD_DIM)
    output = within + before + skip_gain[None, None, :, None] * values.astype(jnp.float32)
    stored = lax.optimization_barrier(output.reshape(length, inner_width).astype(jnp.bfloat16))
    gated = stored.astype(jnp.float32) * jax.nn.silu(gate_input.astype(jnp.float32))
    grouped = gated.reshape(length, groups, inner_width // groups)
    inverse_rms = lax.rsqrt(jnp.mean(grouped * grouped, axis=2, keepdims=True) + 1e-05)
    normed = lax.optimization_barrier(
        ((grouped * inverse_rms).reshape(length, inner_width) * norm_gain[None, :]).astype(
            jnp.bfloat16
        )
    )
    return scattered_sum(normed, out_weight, "tp")


def solution(mesh):
    in_specs = (
        P("ctx", "tp"),
        P("ctx", "tp"),
        P("ctx", None, "tp"),
        P("ctx", "tp"),
        P("tp"),
        P("tp"),
        P(None, "tp"),
        P("tp"),
        P(None, None, "tp"),
        P(None, "tp"),
        P("tp"),
        P("tp", None),
    )
    out_specs = P(("ctx", "tp"), None)
    return jax.shard_map(local, mesh=mesh, in_specs=in_specs, out_specs=out_specs, check_vma=False)
```

```python
import jax
import jax.numpy as jnp
from jax import lax
from jax.sharding import PartitionSpec as P

HEAD_DIM = 64
STATE = 128
CONV = 4
BLOCK = 128


def passed_along(value, axis, steps):
    count = lax.axis_size(axis)
    first, last = (max(0, -steps), min(count, count - steps))
    return lax.ppermute(value, axis, [(source, source + steps) for source in range(first, last)])


def exclusive_scan(log_total, state, axis):
    count = lax.axis_size(axis)
    heads = state.shape[0]
    rows, cols = state.shape[1:]
    window_log, window_state = log_total, state
    prior_log = jnp.zeros_like(log_total)
    prior_state = jnp.zeros_like(state)
    distance = 1
    while distance < count:
        pairs = [(source, source + distance) for source in range(count - distance)]
        high = window_log.astype(jnp.bfloat16)
        low = (window_log - high.astype(jnp.float32)).astype(jnp.bfloat16)
        log_rows = jnp.pad(jnp.stack([high, low], axis=1), ((0, rows - heads), (0, cols - 2)))
        packed = jnp.concatenate([window_state.astype(jnp.bfloat16), log_rows[None]], axis=0)
        got = lax.ppermute(packed, axis, pairs)
        got_state = got[:heads].astype(jnp.float32)
        got_log = got[heads, :heads, 0].astype(jnp.float32) + got[heads, :heads, 1].astype(jnp.float32)
        prior_state = jnp.exp(prior_log)[:, None, None] * got_state + prior_state
        prior_log = got_log + prior_log
        if 2 * distance < count:
            window_state = jnp.exp(window_log)[:, None, None] * got_state + window_state
            window_log = got_log + window_log
        distance *= 2
    return prior_log, prior_state


def scattered_sum(rows, weight, axis):
    count = lax.axis_size(axis)
    chips = count // 2
    place = lax.axis_index(axis)
    core = place % 2
    chip = place // 2
    length = rows.shape[0]
    share = length // count
    half = weight.shape[1] // 2
    blocks = rows.reshape(chips, 2, share, rows.shape[1])
    sent_rows = lax.dynamic_index_in_dim(blocks, 1 - core, 1, False)
    kept_rows = lax.dynamic_index_in_dim(blocks, core, 1, False)
    swap = [(source, source ^ 1) for source in range(count)]

    half_width = weight.shape[1] // 2
    halves = lax.optimization_barrier((weight[:, :half_width], weight[:, half_width:]))

    def summed_half(columns):
        part = halves[0] if columns.start == 0 else halves[1]
        sent = jnp.einsum("ysk,kd->ysd", sent_rows, part, preferred_element_type=jnp.float32)
        swapped = lax.ppermute(sent.astype(jnp.bfloat16), axis, swap)
        kept = lax.optimization_barrier(
            jnp.einsum("ysk,kd->ysd", kept_rows, part, preferred_element_type=jnp.float32)
        )
        return kept + swapped.astype(jnp.float32)

    summed_right = summed_half(slice(0, half))
    summed_left = summed_half(slice(half, 2 * half))
    if chips == 1:
        return jnp.concatenate([summed_right[0], summed_left[0]], axis=1).astype(jnp.bfloat16)
    rightward = [(source, (source + 2) % count) for source in range(count)]
    leftward = [(source, (source - 2) % count) for source in range(count)]
    right_acc = lax.dynamic_index_in_dim(summed_right, (chip - 1) % chips, 0, False)
    left_acc = lax.dynamic_index_in_dim(summed_left, (chip + 1) % chips, 0, False)
    for step in range(chips - 1):
        got_right = lax.ppermute(right_acc.astype(jnp.bfloat16), axis, rightward)
        got_left = lax.ppermute(left_acc.astype(jnp.bfloat16), axis, leftward)
        right_own = lax.dynamic_index_in_dim(summed_right, (chip - 2 - step) % chips, 0, False)
        left_own = lax.dynamic_index_in_dim(summed_left, (chip + 2 + step) % chips, 0, False)
        right_acc = right_own + got_right.astype(jnp.float32)
        left_acc = left_own + got_left.astype(jnp.float32)
    return jnp.concatenate([right_acc, left_acc], axis=1).astype(jnp.bfloat16)


def causal_conv(values, lead_rows, weight, bias_term):
    padded = lax.optimization_barrier(
        jnp.concatenate([lead_rows, values], axis=0).astype(jnp.float32)
    )
    length = values.shape[0]
    accum = jnp.zeros(values.shape, jnp.float32) + bias_term
    for offset in range(weight.shape[0]):
        accum = accum + weight[offset] * padded[offset : offset + length]
    return jax.nn.silu(accum).astype(jnp.bfloat16)


def local(
    ssm_input,
    gate_input,
    state_maps,
    step_size,
    decay_rate,
    skip_gain,
    conv_weight,
    conv_bias,
    map_conv,
    map_bias,
    norm_gain,
    out_weight,
):
    length = ssm_input.shape[0]
    head_count = step_size.shape[1]
    inner_width = ssm_input.shape[1]
    groups = state_maps.shape[2] // STATE
    repeat = head_count // groups
    blocks = length // BLOCK
    map_width = state_maps.shape[1] * state_maps.shape[2]
    lead_both = passed_along(
        jnp.concatenate(
            [
                ssm_input[length - CONV + 1 :],
                state_maps[length - CONV + 1 :].reshape(CONV - 1, map_width),
            ],
            axis=1,
        ),
        "ctx",
        1,
    )
    lead_input = lead_both[:, :inner_width]
    lead_maps = lead_both[:, inner_width:].reshape((CONV - 1,) + state_maps.shape[1:])
    conv_out = causal_conv(ssm_input, lead_input, conv_weight, conv_bias)
    maps_out = causal_conv(state_maps, lead_maps, map_conv, map_bias)
    log_decay = -decay_rate[None, :] * step_size
    running = jnp.cumsum(log_decay.reshape(blocks, BLOCK, head_count), axis=1)
    values = conv_out.reshape(blocks, BLOCK, head_count, HEAD_DIM)
    input_maps = maps_out[:, 0].reshape(blocks, BLOCK, groups, STATE)
    output_maps = maps_out[:, 1].reshape(blocks, BLOCK, groups, STATE)
    block_steps = step_size.reshape(blocks, BLOCK, head_count)
    scores = jnp.einsum(
        "cqgn,csgn->cgqs", output_maps, input_maps, preferred_element_type=jnp.float32
    )
    scores = jnp.broadcast_to(scores[:, :, None], (blocks, groups, repeat, BLOCK, BLOCK)).reshape(
        blocks, head_count, BLOCK, BLOCK
    )
    head_major = jnp.transpose(running, (0, 2, 1))
    gap_log = head_major[:, :, :, None] - head_major[:, :, None, :]
    causal_mask = jnp.tril(jnp.ones((BLOCK, BLOCK), dtype=bool))
    decays = jnp.exp(jnp.where(causal_mask[None, None], gap_log, -1e30))
    step_major = jnp.transpose(block_steps, (0, 2, 1))
    weights = (scores * decays * step_major[:, :, None, :]).astype(jnp.bfloat16)
    within = jnp.einsum("chqs,cshp->cqhp", weights, values, preferred_element_type=jnp.float32)
    to_end = jnp.exp(running[:, -1:, :] - running) * block_steps
    input_heads = jnp.broadcast_to(
        input_maps[:, :, :, None], (blocks, BLOCK, groups, repeat, STATE)
    ).reshape(blocks, BLOCK, head_count, STATE)
    loaded = (input_heads.astype(jnp.float32) * to_end[..., None]).astype(jnp.bfloat16)
    fresh_state = jnp.einsum("cshn,cshp->chnp", loaded, values, preferred_element_type=jnp.float32)
    totals = running[:, -1, :]

    empty_state = jnp.zeros((head_count, STATE, HEAD_DIM), jnp.float32)
    local_enter = []
    carry_state = empty_state
    for block in range(blocks):
        local_enter.append(carry_state)
        carry_state = jnp.exp(totals[block])[:, None, None] * carry_state + fresh_state[block]
    local_end = carry_state
    local_enter = jnp.stack(local_enter)
    device_log = jnp.sum(totals, axis=0)
    before_log, incoming = exclusive_scan(device_log, local_end, "ctx")
    prior_log = jnp.cumsum(totals, axis=0) - totals
    entering = jnp.exp(prior_log)[:, :, None, None] * incoming[None] + local_enter
    carried = entering.astype(jnp.bfloat16).reshape(blocks, groups, repeat, STATE, HEAD_DIM)
    before = jnp.einsum(
        "cqgn,cgrnp->cqgrp", output_maps, carried, preferred_element_type=jnp.float32
    )
    before = jnp.exp(running)[..., None] * before.reshape(blocks, BLOCK, head_count, HEAD_DIM)
    output = within + before + skip_gain[None, None, :, None] * values.astype(jnp.float32)
    stored = lax.optimization_barrier(output.reshape(length, inner_width).astype(jnp.bfloat16))
    gated = stored.astype(jnp.float32) * jax.nn.silu(gate_input.astype(jnp.float32))
    grouped = gated.reshape(length, groups, inner_width // groups)
    inverse_rms = lax.rsqrt(jnp.mean(grouped * grouped, axis=2, keepdims=True) + 1e-05)
    normed = lax.optimization_barrier(
        ((grouped * inverse_rms).reshape(length, inner_width) * norm_gain[None, :]).astype(
            jnp.bfloat16
        )
    )
    return scattered_sum(normed, out_weight, "tp")


def solution(mesh):
    in_specs = (
        P("ctx", "tp"),
        P("ctx", "tp"),
        P("ctx", None, "tp"),
        P("ctx", "tp"),
        P("tp"),
        P("tp"),
        P(None, "tp"),
        P("tp"),
        P(None, None, "tp"),
        P(None, "tp"),
        P("tp"),
        P("tp", None),
    )
    out_specs = P(("ctx", "tp"), None)
    return jax.shard_map(local, mesh=mesh, in_specs=in_specs, out_specs=out_specs, check_vma=False)
```

```python
import jax
import jax.numpy as jnp
from jax import lax
from jax.sharding import PartitionSpec as P

HEAD_DIM = 64
STATE = 128
CONV = 4
BLOCK = 128


def passed_along(value, axis, steps):
    count = lax.axis_size(axis)
    first, last = (max(0, -steps), min(count, count - steps))
    return lax.ppermute(value, axis, [(source, source + steps) for source in range(first, last)])


def exclusive_scan(log_total, state, axis):
    count = lax.axis_size(axis)
    heads = state.shape[0]
    rows, cols = state.shape[1:]
    window_log, window_state = log_total, state
    prior_log = jnp.zeros_like(log_total)
    prior_state = jnp.zeros_like(state)
    distance = 1
    while distance < count:
        pairs = [(source, source + distance) for source in range(count - distance)]
        high = window_log.astype(jnp.bfloat16)
        low = (window_log - high.astype(jnp.float32)).astype(jnp.bfloat16)
        log_rows = jnp.pad(jnp.stack([high, low], axis=1), ((0, rows - heads), (0, cols - 2)))
        packed = jnp.concatenate([window_state.astype(jnp.bfloat16), log_rows[None]], axis=0)
        got = lax.ppermute(packed, axis, pairs)
        got_state = got[:heads].astype(jnp.float32)
        got_log = got[heads, :heads, 0].astype(jnp.float32) + got[heads, :heads, 1].astype(jnp.float32)
        prior_state = jnp.exp(prior_log)[:, None, None] * got_state + prior_state
        prior_log = got_log + prior_log
        if 2 * distance < count:
            window_state = jnp.exp(window_log)[:, None, None] * got_state + window_state
            window_log = got_log + window_log
        distance *= 2
    return prior_log, prior_state


def scattered_sum(rows, weight, axis):
    count = lax.axis_size(axis)
    chips = count // 2
    place = lax.axis_index(axis)
    core = place % 2
    chip = place // 2
    length = rows.shape[0]
    share = length // count
    half = weight.shape[1] // 2
    blocks = rows.reshape(chips, 2, share, rows.shape[1])
    sent_rows = lax.dynamic_index_in_dim(blocks, 1 - core, 1, False)
    kept_rows = lax.dynamic_index_in_dim(blocks, core, 1, False)
    swap = [(source, source ^ 1) for source in range(count)]

    def summed_half(columns):
        part = weight[:, columns]
        sent = jnp.einsum("ysk,kd->ysd", sent_rows, part, preferred_element_type=jnp.float32)
        swapped = lax.ppermute(sent.astype(jnp.bfloat16), axis, swap)
        kept = lax.optimization_barrier(
            jnp.einsum("ysk,kd->ysd", kept_rows, part, preferred_element_type=jnp.float32)
        )
        return kept + swapped.astype(jnp.float32)

    summed_right = summed_half(slice(0, half))
    summed_left = summed_half(slice(half, 2 * half))
    if chips == 1:
        return jnp.concatenate([summed_right[0], summed_left[0]], axis=1).astype(jnp.bfloat16)
    rightward = [(source, (source + 2) % count) for source in range(count)]
    leftward = [(source, (source - 2) % count) for source in range(count)]
    right_acc = lax.dynamic_index_in_dim(summed_right, (chip - 1) % chips, 0, False)
    left_acc = lax.dynamic_index_in_dim(summed_left, (chip + 1) % chips, 0, False)
    for step in range(chips - 1):
        got_right = lax.ppermute(right_acc.astype(jnp.bfloat16), axis, rightward)
        got_left = lax.ppermute(left_acc.astype(jnp.bfloat16), axis, leftward)
        right_own = lax.dynamic_index_in_dim(summed_right, (chip - 2 - step) % chips, 0, False)
        left_own = lax.dynamic_index_in_dim(summed_left, (chip + 2 + step) % chips, 0, False)
        right_acc = right_own + got_right.astype(jnp.float32)
        left_acc = left_own + got_left.astype(jnp.float32)
    return jnp.concatenate([right_acc, left_acc], axis=1).astype(jnp.bfloat16)


def causal_conv(values, lead_rows, weight, bias_term):
    padded = lax.optimization_barrier(
        jnp.concatenate([lead_rows, values], axis=0).astype(jnp.float32)
    )
    length = values.shape[0]
    accum = jnp.zeros(values.shape, jnp.float32) + bias_term
    for offset in range(weight.shape[0]):
        accum = accum + weight[offset] * padded[offset : offset + length]
    return jax.nn.silu(accum).astype(jnp.bfloat16)


def local(
    ssm_input,
    gate_input,
    state_maps,
    step_size,
    decay_rate,
    skip_gain,
    conv_weight,
    conv_bias,
    map_conv,
    map_bias,
    norm_gain,
    out_weight,
):
    length = ssm_input.shape[0]
    head_count = step_size.shape[1]
    inner_width = ssm_input.shape[1]
    groups = state_maps.shape[2] // STATE
    repeat = head_count // groups
    blocks = length // BLOCK
    map_width = state_maps.shape[1] * state_maps.shape[2]
    lead_both = passed_along(
        jnp.concatenate(
            [
                ssm_input[length - CONV + 1 :],
                state_maps[length - CONV + 1 :].reshape(CONV - 1, map_width),
            ],
            axis=1,
        ),
        "ctx",
        1,
    )
    lead_input = lead_both[:, :inner_width]
    lead_maps = lead_both[:, inner_width:].reshape((CONV - 1,) + state_maps.shape[1:])
    conv_out = causal_conv(ssm_input, lead_input, conv_weight, conv_bias)
    maps_out = causal_conv(state_maps, lead_maps, map_conv, map_bias)
    log_decay = -decay_rate[None, :] * step_size
    running = jnp.cumsum(log_decay.reshape(blocks, BLOCK, head_count), axis=1)
    values = conv_out.reshape(blocks, BLOCK, head_count, HEAD_DIM)
    input_maps = maps_out[:, 0].reshape(blocks, BLOCK, groups, STATE)
    output_maps = maps_out[:, 1].reshape(blocks, BLOCK, groups, STATE)
    block_steps = step_size.reshape(blocks, BLOCK, head_count)
    scores = jnp.einsum(
        "cqgn,csgn->cgqs", output_maps, input_maps, preferred_element_type=jnp.float32
    )
    scores = jnp.broadcast_to(scores[:, :, None], (blocks, groups, repeat, BLOCK, BLOCK)).reshape(
        blocks, head_count, BLOCK, BLOCK
    )
    head_major = jnp.transpose(running, (0, 2, 1))
    gap_log = head_major[:, :, :, None] - head_major[:, :, None, :]
    causal_mask = jnp.tril(jnp.ones((BLOCK, BLOCK), dtype=bool))
    decays = jnp.exp(jnp.where(causal_mask[None, None], gap_log, -1e30))
    step_major = jnp.transpose(block_steps, (0, 2, 1))
    weights = (scores * decays * step_major[:, :, None, :]).astype(jnp.bfloat16)
    within = jnp.einsum("chqs,cshp->cqhp", weights, values, preferred_element_type=jnp.float32)
    to_end = jnp.exp(running[:, -1:, :] - running) * block_steps
    input_heads = jnp.broadcast_to(
        input_maps[:, :, :, None], (blocks, BLOCK, groups, repeat, STATE)
    ).reshape(blocks, BLOCK, head_count, STATE)
    loaded = (input_heads.astype(jnp.float32) * to_end[..., None]).astype(jnp.bfloat16)
    fresh_state = jnp.einsum("cshn,cshp->chnp", loaded, values, preferred_element_type=jnp.float32)
    totals = running[:, -1, :]

    empty_state = jnp.zeros((head_count, STATE, HEAD_DIM), jnp.float32)
    local_enter = []
    carry_state = empty_state
    for block in range(blocks):
        local_enter.append(carry_state)
        carry_state = jnp.exp(totals[block])[:, None, None] * carry_state + fresh_state[block]
    local_end = carry_state
    local_enter = jnp.stack(local_enter)
    device_log = jnp.sum(totals, axis=0)
    before_log, incoming = exclusive_scan(device_log, local_end, "ctx")
    prior_log = jnp.cumsum(totals, axis=0) - totals
    entering = jnp.exp(prior_log)[:, :, None, None] * incoming[None] + local_enter
    carried = entering.astype(jnp.bfloat16).reshape(blocks, groups, repeat, STATE, HEAD_DIM)
    before = jnp.einsum(
        "cqgn,cgrnp->cqgrp", output_maps, carried, preferred_element_type=jnp.float32
    )
    before = jnp.exp(running)[..., None] * before.reshape(blocks, BLOCK, head_count, HEAD_DIM)
    output = before + lax.optimization_barrier(
        (within + skip_gain[None, None, :, None] * values.astype(jnp.float32)).astype(jnp.bfloat16)
    ).astype(jnp.float32)
    stored = lax.optimization_barrier(output.reshape(length, inner_width).astype(jnp.bfloat16))
    gated = stored.astype(jnp.float32) * jax.nn.silu(gate_input.astype(jnp.float32))
    grouped = gated.reshape(length, groups, inner_width // groups)
    inverse_rms = lax.rsqrt(jnp.mean(grouped * grouped, axis=2, keepdims=True) + 1e-05)
    normed = lax.optimization_barrier(
        ((grouped * inverse_rms).reshape(length, inner_width) * norm_gain[None, :]).astype(
            jnp.bfloat16
        )
    )
    return scattered_sum(normed, out_weight, "tp")


def solution(mesh):
    in_specs = (
        P("ctx", "tp"),
        P("ctx", "tp"),
        P("ctx", None, "tp"),
        P("ctx", "tp"),
        P("tp"),
        P("tp"),
        P(None, "tp"),
        P("tp"),
        P(None, None, "tp"),
        P(None, "tp"),
        P("tp"),
        P("tp", None),
    )
    out_specs = P(("ctx", "tp"), None)
    return jax.shard_map(local, mesh=mesh, in_specs=in_specs, out_specs=out_specs, check_vma=False)
```

```python
import jax
import jax.numpy as jnp
from jax import lax
from jax.sharding import PartitionSpec as P

HEAD_DIM = 64
STATE = 128
CONV = 4
BLOCK = 128


def passed_along(value, axis, steps):
    count = lax.axis_size(axis)
    first, last = (max(0, -steps), min(count, count - steps))
    return lax.ppermute(value, axis, [(source, source + steps) for source in range(first, last)])


def exclusive_scan(log_total, state, axis):
    count = lax.axis_size(axis)
    heads = state.shape[0]
    rows, cols = state.shape[1:]
    window_log, window_state = log_total, state
    prior_log = jnp.zeros_like(log_total)
    prior_state = jnp.zeros_like(state)
    distance = 1
    while distance < count:
        pairs = [(source, source + distance) for source in range(count - distance)]
        high = window_log.astype(jnp.bfloat16)
        low = (window_log - high.astype(jnp.float32)).astype(jnp.bfloat16)
        log_rows = jnp.pad(jnp.stack([high, low], axis=1), ((0, rows - heads), (0, cols - 2)))
        packed = jnp.concatenate([window_state.astype(jnp.bfloat16), log_rows[None]], axis=0)
        got = lax.ppermute(packed, axis, pairs)
        got_state = got[:heads].astype(jnp.float32)
        got_log = got[heads, :heads, 0].astype(jnp.float32) + got[heads, :heads, 1].astype(jnp.float32)
        prior_state = jnp.exp(prior_log)[:, None, None] * got_state + prior_state
        prior_log = got_log + prior_log
        if 2 * distance < count:
            window_state = jnp.exp(window_log)[:, None, None] * got_state + window_state
            window_log = got_log + window_log
        distance *= 2
    return prior_log, prior_state


def scattered_sum(rows, weight, axis):
    count = lax.axis_size(axis)
    chips = count // 2
    place = lax.axis_index(axis)
    core = place % 2
    chip = place // 2
    length = rows.shape[0]
    share = length // count
    half = weight.shape[1] // 2
    blocks = rows.reshape(chips, 2, share, rows.shape[1])
    sent_rows = lax.dynamic_index_in_dim(blocks, 1 - core, 1, False)
    kept_rows = lax.dynamic_index_in_dim(blocks, core, 1, False)
    swap = [(source, source ^ 1) for source in range(count)]

    def summed_half(columns):
        part = weight[:, columns]
        sent = jnp.einsum("ysk,kd->ysd", sent_rows, part, preferred_element_type=jnp.float32)
        swapped = lax.ppermute(sent.astype(jnp.bfloat16), axis, swap)
        kept = lax.optimization_barrier(
            jnp.einsum("ysk,kd->ysd", kept_rows, part, preferred_element_type=jnp.float32)
        )
        return kept + swapped.astype(jnp.float32)

    summed_right = summed_half(slice(0, half))
    summed_left = summed_half(slice(half, 2 * half))
    if chips == 1:
        return jnp.concatenate([summed_right[0], summed_left[0]], axis=1).astype(jnp.bfloat16)
    rightward = [(source, (source + 2) % count) for source in range(count)]
    leftward = [(source, (source - 2) % count) for source in range(count)]
    right_acc = lax.dynamic_index_in_dim(summed_right, (chip - 1) % chips, 0, False)
    left_acc = lax.dynamic_index_in_dim(summed_left, (chip + 1) % chips, 0, False)
    for step in range(chips - 1):
        got_right = lax.ppermute(right_acc.astype(jnp.bfloat16), axis, rightward)
        got_left = lax.ppermute(left_acc.astype(jnp.bfloat16), axis, leftward)
        right_own = lax.dynamic_index_in_dim(summed_right, (chip - 2 - step) % chips, 0, False)
        left_own = lax.dynamic_index_in_dim(summed_left, (chip + 2 + step) % chips, 0, False)
        right_acc = right_own + got_right.astype(jnp.float32)
        left_acc = left_own + got_left.astype(jnp.float32)
    return jnp.concatenate([right_acc, left_acc], axis=1).astype(jnp.bfloat16)


def causal_conv(values, lead_rows, weight, bias_term):
    padded = lax.optimization_barrier(
        jnp.concatenate([lead_rows, values], axis=0).astype(jnp.float32)
    )
    length = values.shape[0]
    accum = jnp.zeros(values.shape, jnp.float32) + bias_term
    for offset in range(weight.shape[0]):
        accum = accum + weight[offset] * padded[offset : offset + length]
    return jax.nn.silu(accum).astype(jnp.bfloat16)


def local(
    ssm_input,
    gate_input,
    state_maps,
    step_size,
    decay_rate,
    skip_gain,
    conv_weight,
    conv_bias,
    map_conv,
    map_bias,
    norm_gain,
    out_weight,
):
    length = ssm_input.shape[0]
    head_count = step_size.shape[1]
    inner_width = ssm_input.shape[1]
    groups = state_maps.shape[2] // STATE
    repeat = head_count // groups
    blocks = length // BLOCK
    map_width = state_maps.shape[1] * state_maps.shape[2]
    lead_both = passed_along(
        jnp.concatenate(
            [
                ssm_input[length - CONV + 1 :],
                state_maps[length - CONV + 1 :].reshape(CONV - 1, map_width),
            ],
            axis=1,
        ),
        "ctx",
        1,
    )
    lead_input = lead_both[:, :inner_width]
    lead_maps = lead_both[:, inner_width:].reshape((CONV - 1,) + state_maps.shape[1:])
    conv_out = causal_conv(ssm_input, lead_input, conv_weight, conv_bias)
    maps_out = causal_conv(state_maps, lead_maps, map_conv, map_bias)
    log_decay = -decay_rate[None, :] * step_size
    running = jnp.cumsum(log_decay.reshape(blocks, BLOCK, head_count), axis=1)
    values = conv_out.reshape(blocks, BLOCK, head_count, HEAD_DIM)
    input_maps = maps_out[:, 0].reshape(blocks, BLOCK, groups, STATE)
    output_maps = maps_out[:, 1].reshape(blocks, BLOCK, groups, STATE)
    block_steps = step_size.reshape(blocks, BLOCK, head_count)
    scores = jnp.einsum(
        "cqgn,csgn->cgqs", output_maps, input_maps, preferred_element_type=jnp.float32
    )
    scores = jnp.broadcast_to(scores[:, :, None], (blocks, groups, repeat, BLOCK, BLOCK)).reshape(
        blocks, head_count, BLOCK, BLOCK
    )
    head_major = jnp.transpose(running, (0, 2, 1))
    gap_log = head_major[:, :, :, None] - head_major[:, :, None, :]
    causal_mask = jnp.tril(jnp.ones((BLOCK, BLOCK), dtype=bool))
    decays = jnp.exp(jnp.where(causal_mask[None, None], gap_log, -1e30))
    step_major = jnp.transpose(block_steps, (0, 2, 1))
    weights = (scores * decays * step_major[:, :, None, :]).astype(jnp.bfloat16)
    within = jnp.einsum("chqs,cshp->cqhp", weights, values, preferred_element_type=jnp.float32)
    to_end = jnp.exp(running[:, -1:, :] - running) * block_steps
    input_heads = jnp.broadcast_to(
        input_maps[:, :, :, None], (blocks, BLOCK, groups, repeat, STATE)
    ).reshape(blocks, BLOCK, head_count, STATE)
    loaded = (input_heads.astype(jnp.float32) * to_end[..., None]).astype(jnp.bfloat16)
    fresh_state = jnp.einsum("cshn,cshp->chnp", loaded, values, preferred_element_type=jnp.float32)
    totals = running[:, -1, :]

    empty_state = jnp.zeros((head_count, STATE, HEAD_DIM), jnp.float32)
    local_enter = []
    carry_state = empty_state
    for block in range(blocks):
        local_enter.append(carry_state)
        carry_state = jnp.exp(totals[block])[:, None, None] * carry_state + fresh_state[block]
    local_end = carry_state
    local_enter = jnp.stack(local_enter)
    device_log = jnp.sum(totals, axis=0)
    before_log, incoming = exclusive_scan(device_log, local_end, "ctx")
    prior_log = jnp.cumsum(totals, axis=0) - totals
    entering = jnp.exp(prior_log)[:, :, None, None] * incoming[None] + local_enter
    carried = entering.astype(jnp.bfloat16).reshape(blocks, groups, repeat, STATE, HEAD_DIM)
    before = jnp.einsum(
        "cqgn,cgrnp->cqgrp", output_maps, carried, preferred_element_type=jnp.float32
    )
    before = jnp.exp(running)[..., None] * before.reshape(blocks, BLOCK, head_count, HEAD_DIM)
    output = before + lax.optimization_barrier(
        (within + skip_gain[None, None, :, None] * values.astype(jnp.float32)).astype(jnp.bfloat16)
    ).astype(jnp.float32)
    stored = lax.optimization_barrier(output.reshape(length, inner_width).astype(jnp.bfloat16))
    gate_scale = lax.optimization_barrier(jax.nn.silu(gate_input.astype(jnp.float32)).astype(jnp.bfloat16))
    gated = stored.astype(jnp.float32) * gate_scale.astype(jnp.float32)
    grouped = gated.reshape(length, groups, inner_width // groups)
    inverse_rms = lax.rsqrt(jnp.mean(grouped * grouped, axis=2, keepdims=True) + 1e-05)
    normed = lax.optimization_barrier(
        ((grouped * inverse_rms).reshape(length, inner_width) * norm_gain[None, :]).astype(
            jnp.bfloat16
        )
    )
    return scattered_sum(normed, out_weight, "tp")


def solution(mesh):
    in_specs = (
        P("ctx", "tp"),
        P("ctx", "tp"),
        P("ctx", None, "tp"),
        P("ctx", "tp"),
        P("tp"),
        P("tp"),
        P(None, "tp"),
        P("tp"),
        P(None, None, "tp"),
        P(None, "tp"),
        P("tp"),
        P("tp", None),
    )
    out_specs = P(("ctx", "tp"), None)
    return jax.shard_map(local, mesh=mesh, in_specs=in_specs, out_specs=out_specs, check_vma=False)
```
